512 devices in a mesh: kv: 8 (over y, core), pages: 64 (over x, z).
Axes of the slice: x: 4, y: 4, z: 16, core: 2. Of those that a mesh axis runs over, the one named last changes fastest.
Arguments:
- tokens: int32 [2, 64], replicated, may hold values from 0 to 31999
- prompt_len: int32 [8], replicated, may hold values from 193 to 8192, as said below
- page_table: int32 [8, 64], replicated, may hold values from -1 to 511, as said below
- parents: int32 [2, 64], replicated, may hold values from 0 to 63, as said below
- embedding: bfloat16 [32000, 7168], P('kv', 'pages'), may hold values from -6 to 6
- norm_gain: bfloat16 [7168], P('pages'), may hold values from 0.099609375 to 1.8984375
- w_qkv: bfloat16 [7168, 9216], P('pages', 'kv'), may hold values from -0.0625 to 0.0625
- w_out: bfloat16 [7168, 7168], P('kv', 'pages'), may hold values from -0.8984375 to 0.8984375
- history: bfloat16 [2, 64, 13, 1024], P(None, None, None, 'kv'), may hold values from -6 to 6
- kv_pool: bfloat16 [2, 512, 128, 1024], P(None, 'pages', None, 'kv'), may hold values from -400 to 400
Outputs:
- hidden: bfloat16 [2, 64, 7168], P(None, None, 'pages')
- history_out: bfloat16 [2, 64, 15, 1024], P(None, None, None, 'kv')
The draws below stay inside these ranges and needn't reach their ends.
Inputs may be any that keep to these rules, and one draw needn't show every extreme that they name: `prompt_len`: each prompt is either long, within 512 tokens below 8192, or short, within 64 tokens below 256; some group's prompt has exactly 8192 tokens. For j below prompt_len[g] / 128 rounded up, page_table[g, j] is the slot holding tokens j * 128 to j * 128 + 127 of group g's prompt; no slot is named twice; all other entries are -1. parents[t, b] is a beam of b's group; at the first step the first and the last beam of every group continue their own history.
All inputs are finite; a program needn't handle non-finite values.
Results may differ from the reference program's by a relative error of at most 0.015.
The reference program's roundings to bfloat16 on the way count: a program that leaves them out, or rounds other values in their place, can miss the bound.
Values may be sent and summed in bfloat16 or wider, within the bound.
No kernel may reach another device: no remote copies, remote signals or barrier semaphores. Data moves between devices by JAX's collectives and lax.ppermute only.
A program may use at most 128 MiB of HBM per device.

```python
import math
import jax
import jax.numpy as jnp
import numpy as np
from jax import lax

D = 7168
HEADS = 56
KV_HEADS = 8
HEAD_DIM = 128
VOCAB = 32000
GROUPS = 8
BEAMS = 8
STEPS = 2
PRIOR = 13
MAXLEN = 8192
SHORT = 256
PAGE = 128
PER_KV = 7
SEQS = 64
HISTORY = 15
MAX_PAGES = 64
SLOTS_ALL = 512


def prompt_plan(key):
    base_key = jax.random.fold_in(key, 7)
    key_kind, key_long, key_short, key_most, key_order = jax.random.split(base_key, 5)
    is_long = jax.random.randint(key_kind, (GROUPS,), 0, 2)
    long_len = MAXLEN - jax.random.randint(key_long, (GROUPS,), 0, MAXLEN // 16)
    short_len = SHORT - jax.random.randint(key_short, (GROUPS,), 0, SHORT // 4)
    lengths = jnp.where(is_long == 1, long_len, short_len)
    longest = jax.random.randint(key_most, (), 0, GROUPS)
    lengths = jnp.where(jnp.arange(GROUPS) == longest, MAXLEN, lengths)
    page_count = (lengths + PAGE - 1) // PAGE
    page_start = jnp.cumsum(page_count) - page_count
    shuffled = jax.random.permutation(key_order, SLOTS_ALL)
    column = jnp.arange(MAX_PAGES)
    index_all = jnp.clip(page_start[:, None] + column[None, :], 0, SLOTS_ALL - 1)
    table_out = jnp.where(column[None, :] < page_count[:, None], shuffled[index_all], -1)
    return (lengths.astype(jnp.int32), table_out.astype(jnp.int32))


def draw_prompt_len(key, part):
    return prompt_plan(key)[0]


def draw_page_table(key, part):
    return prompt_plan(key)[1]


def draw_parents(key, part):
    pick_key = jax.random.fold_in(key, 11)
    beam_ids = jnp.arange(SEQS)
    pick = jax.random.randint(pick_key, (STEPS, SEQS), 0, BEAMS)
    chosen = beam_ids // BEAMS * BEAMS + pick
    keep_own = (beam_ids % BEAMS == 0) | (beam_ids % BEAMS == BEAMS - 1)
    first_row = jnp.where(keep_own, beam_ids, chosen[0])
    chosen = chosen.at[0].set(first_row)
    return chosen.astype(jnp.int32)


def draw_kv_pool(key, part):
    base_key = jax.random.fold_in(key, 13)
    key_main = jax.random.fold_in(base_key, 0)
    shape_all = (2, SLOTS_ALL, PAGE, KV_HEADS * HEAD_DIM)
    values = jnp.clip(jax.random.normal(key_main, shape_all, jnp.float32), -6.0, 6.0)
    return values.astype(jnp.bfloat16)


def plant(values, own_key, least, high):
    shape = values.shape
    index_at = [jax.random.randint(jax.random.fold_in(own_key, axis), (), 0, shape[axis]) for axis in range(len(shape))]
    values = values.at[tuple(index_at)].set(least)
    longest = shape.index(max(shape))
    index_at[longest] = (index_at[longest] + 1) % shape[longest]
    return values.at[tuple(index_at)].set(high)


def block_scale(own_key, shape, cuts, least, largest):
    level, own = 1.0, jax.random.fold_in(own_key, 6)
    for dim, blocks in cuts:
        heights = jnp.exp(jax.random.uniform(jax.random.fold_in(own, dim), (blocks,), jnp.float32, least / len(cuts), largest / len(cuts)))
        level = level * jnp.repeat(heights, shape[dim] // blocks).reshape([-1 if axis == dim else 1 for axis in range(len(shape))])
    return level


def cumulative_ranks(count, skew):
    portions = [(1 << 20) // math.isqrt(rank ** skew) + 1 for rank in range(1, count + 1)]
    width = 1 + sum(portions) // (1 << 30)
    return np.cumsum(np.array([max(1, weight // width) for weight in portions]))


def ranked(key, shape, amount, skew):
    grid = cumulative_ranks(amount, skew)
    ticket = jax.random.randint(jax.random.fold_in(key, 1), shape, 0, int(grid[amount - 1]))
    rank = jnp.searchsorted(jnp.asarray(grid, jnp.int32), ticket, side="right")
    return jax.random.permutation(jax.random.fold_in(key, 2), amount)[rank].astype(jnp.int32)


def scatter_about(rng, extent, spread, bound, shards=(), kind=jnp.bfloat16):
    factor_of = block_scale(rng, extent, shards, -0.22, 0.18) if shards else 1.0
    entries = jax.random.normal(rng, extent, jnp.float32) * spread * factor_of
    return jnp.minimum(jnp.maximum(entries, -bound), bound).astype(kind)


def setup_inputs(seed: int = 0) -> dict:
    key_of = jax.random.split(jax.random.key(seed), 11)
    return {
        "tokens": plant(ranked(key_of[0], (STEPS, SEQS), VOCAB, 2), jax.random.fold_in(key_of[0], 3), 0, VOCAB - 1).astype(jnp.int32),
        "prompt_len": draw_prompt_len(jax.random.fold_in(key_of[10], 71), 0),
        "page_table": draw_page_table(jax.random.fold_in(key_of[10], 71), 0),
        "parents": draw_parents(jax.random.fold_in(key_of[10], 71), 0),
        "embedding": scatter_about(key_of[4], (VOCAB, D), 1.0, 6.0, ((0, 8), (1, 64))),
        "norm_gain": jnp.clip(1.0 + 0.18 * jax.random.normal(key_of[5], (D,), jnp.float32), 0.099609375, 1.8984375).astype(jnp.bfloat16),
        "w_qkv": scatter_about(key_of[6], (D, KV_HEADS * (PER_KV + 2) * HEAD_DIM), D ** -0.5, 0.0625, ((0, 64), (1, 8))),
        "w_out": scatter_about(key_of[7], (HEADS * HEAD_DIM, D), 0.15, 0.8984375, ((0, 8), (1, 64))),
        "history": scatter_about(key_of[8], (2, SEQS, PRIOR, KV_HEADS * HEAD_DIM), 1.0, 6.0, ((3, 8),)),
        "kv_pool": draw_kv_pool(jax.random.fold_in(key_of[10], 71), 0),
    }


THETA = 5000000.0
EPSILON = 1e-05
NEGATIVE = -1e+30

def rotate(values, positions):
    half_dim = HEAD_DIM // 2
    frequency = THETA ** (-(2.0 * jnp.arange(half_dim, dtype=jnp.float32)) / HEAD_DIM)
    angles = positions.astype(jnp.float32)[:, None] * frequency[None, :]
    cosine = jnp.cos(angles)[:, None, None, :]
    sine_part = jnp.sin(angles)[:, None, None, :]
    lower_part = values[..., :half_dim]
    upper_part = values[..., half_dim:]
    return jnp.concatenate([lower_part * cosine - upper_part * sine_part, upper_part * cosine + lower_part * sine_part], axis=-1)

def reference(tokens, prompt_len, page_table, parents, embedding, norm_gain, w_qkv, w_out, history, kv_pool):
    num_seqs = GROUPS * BEAMS
    row_count = STEPS * num_seqs
    kv_width = KV_HEADS * HEAD_DIM
    embedded = jnp.take(embedding, tokens.reshape(-1).astype(jnp.int32), axis=0)
    widened = embedded.astype(jnp.float32)
    inverse_rms = lax.rsqrt(lax.optimization_barrier(jnp.mean(widened * widened, axis=1)) + EPSILON)
    normed = (widened * norm_gain.astype(jnp.float32)).astype(jnp.bfloat16)
    projected = jnp.dot(normed, w_qkv, preferred_element_type=jnp.float32) * inverse_rms[:, None]
    projected = projected.reshape(row_count, KV_HEADS, PER_KV + 2, HEAD_DIM)
    row_ids = jnp.arange(row_count, dtype=jnp.int32)
    positions = jnp.take(prompt_len, row_ids % num_seqs // BEAMS) + PRIOR + row_ids // num_seqs
    turned = rotate(projected[:, :, :PER_KV + 1], positions)
    queries = turned[:, :, :PER_KV].astype(jnp.bfloat16)
    queries = queries.reshape(STEPS, GROUPS, BEAMS, KV_HEADS, PER_KV, HEAD_DIM)
    fresh_kv = jnp.stack([turned[:, :, PER_KV], projected[:, :, PER_KV + 1]]).astype(jnp.bfloat16)
    fresh_kv = fresh_kv.reshape(2, STEPS, num_seqs, kv_width)
    buffer = jnp.concatenate([history, jnp.zeros((2, num_seqs, STEPS, kv_width), jnp.bfloat16)], axis=2)
    snapshots = []
    for step_index in range(STEPS):
        buffer = jnp.take(buffer, parents[step_index].astype(jnp.int32), axis=1)
        buffer = buffer.at[:, :, PRIOR + step_index].set(fresh_kv[:, step_index])
        snapshots.append(buffer)
    stacked = jnp.stack(snapshots).reshape(STEPS, 2, GROUPS, BEAMS, HISTORY, KV_HEADS, HEAD_DIM)
    tail_len = PRIOR + 1 + jnp.arange(STEPS, dtype=jnp.int32)
    tail_valid = jnp.arange(HISTORY, dtype=jnp.int32)[None, :] < tail_len[:, None]
    pool_keys = kv_pool[0].reshape(SLOTS_ALL, PAGE, KV_HEADS, HEAD_DIM)
    pool_vals = kv_pool[1].reshape(SLOTS_ALL, PAGE, KV_HEADS, HEAD_DIM)
    root = jnp.sqrt(jnp.float32(HEAD_DIM))

    def one_group(group):
        slot_list = jnp.clip(page_table[group], 0, SLOTS_ALL - 1).astype(jnp.int32)
        group_keys = jnp.take(pool_keys, slot_list, axis=0).reshape(MAXLEN, KV_HEADS, HEAD_DIM).astype(jnp.float32)
        group_vals = jnp.take(pool_vals, slot_list, axis=0).reshape(MAXLEN, KV_HEADS, HEAD_DIM).astype(jnp.float32)
        group_query = lax.dynamic_index_in_dim(queries, group, axis=1, keepdims=False).astype(jnp.float32)
        tail_group = lax.dynamic_index_in_dim(stacked, group, axis=2, keepdims=False).astype(jnp.float32)
        prompt_scores = jnp.einsum('tbkhd,lkd->tbkhl', group_query, group_keys) / root
        live_tok = jnp.arange(MAXLEN, dtype=jnp.int32) < prompt_len[group]
        prompt_scores = jnp.where(live_tok, prompt_scores, NEGATIVE)
        tail_scores = jnp.einsum('tbkhd,tblkd->tbkhl', group_query, tail_group[:, 0]) / root
        tail_scores = jnp.where(tail_valid[:, None, None, None, :], tail_scores, NEGATIVE)
        peak = jnp.maximum(lax.optimization_barrier(jnp.max(prompt_scores, axis=-1)), lax.optimization_barrier(jnp.max(tail_scores, axis=-1)))
        prompt_exp = jnp.where(live_tok, jnp.exp(prompt_scores - peak[..., None]), 0.0)
        tail_exp = jnp.where(tail_valid[:, None, None, None, :], jnp.exp(tail_scores - peak[..., None]), 0.0)
        denominator = lax.optimization_barrier(jnp.sum(prompt_exp, axis=-1)) + lax.optimization_barrier(jnp.sum(tail_exp, axis=-1))
        prompt_w = lax.optimization_barrier(prompt_exp.astype(jnp.bfloat16)).astype(jnp.float32)
        tail_w = lax.optimization_barrier(tail_exp.astype(jnp.bfloat16)).astype(jnp.float32)
        numerator = jnp.einsum('tbkhl,lkd->tbkhd', prompt_w, group_vals)
        numerator = numerator + jnp.einsum('tbkhl,tblkd->tbkhd', tail_w, tail_group[:, 1])
        return (numerator / denominator[..., None]).astype(jnp.bfloat16)
    attended = lax.map(one_group, jnp.arange(GROUPS, dtype=jnp.int32))
    attended = jnp.moveaxis(attended, 0, 1).reshape(row_count, KV_HEADS * PER_KV * HEAD_DIM)
    mixed_out = jnp.dot(attended, w_out, preferred_element_type=jnp.float32) + widened
    hidden = mixed_out.astype(jnp.bfloat16).reshape(STEPS, num_seqs, D)
    return (hidden, buffer)
```

```python
import jax
import jax.numpy as jnp
from jax import lax
from jax.sharding import PartitionSpec as P

D = 7168
KV_HEADS = 8
HEAD_DIM = 128
GROUPS = 8
BEAMS = 8
PRIOR = 13
PAGE = 128
PER_KV = 7
HISTORY = 15
MAX_PAGES = 64


THETA = 5000000.0
EPSILON = 1e-05
NEGATIVE = -1e30


def rotate(values, positions):
    half_dim = HEAD_DIM // 2
    frequency = THETA ** (-(2.0 * jnp.arange(half_dim, dtype=jnp.float32)) / HEAD_DIM)
    angles = positions.astype(jnp.float32)[:, None] * frequency[None, :]
    cosine = jnp.cos(angles)[:, None, None, :]
    sine_part = jnp.sin(angles)[:, None, None, :]
    lower_part = values[..., :half_dim]
    upper_part = values[..., half_dim:]
    return jnp.concatenate(
        [
            lower_part * cosine - upper_part * sine_part,
            upper_part * cosine + lower_part * sine_part,
        ],
        axis=-1,
    )


def finish_rows(summed, norm_sums, row_ids, prompt_len, num_seqs, local_heads):
    inverse_rms = lax.rsqrt(norm_sums / D + EPSILON)
    projected = (summed * inverse_rms[:, None]).reshape(-1, local_heads, PER_KV + 2, HEAD_DIM)
    positions = jnp.take(prompt_len, row_ids % num_seqs // BEAMS) + PRIOR + row_ids // num_seqs
    turned = rotate(projected[:, :, : PER_KV + 1], positions)
    return jnp.concatenate([turned, projected[:, :, PER_KV + 1 :]], axis=2).astype(jnp.bfloat16)


def combine(earlier, later):
    peak = jnp.maximum(earlier[0], later[0])
    weight_one = jnp.exp(earlier[0] - peak)
    weight_two = jnp.exp(later[0] - peak)
    return (
        peak,
        earlier[1] * weight_one + later[1] * weight_two,
        earlier[2] * weight_one[:, None] + later[2] * weight_two[:, None],
    )


def reduce_rows(packed, axis):
    sources = lax.axis_size(axis)
    split = packed.reshape(sources, packed.shape[0] // sources, *packed.shape[1:])
    return jnp.sum(lax.all_to_all(split, axis, 0, 0, tiled=False), axis=0)


def per_device(
    tokens, prompt_len, page_table, parents, embedding, norm_gain, w_qkv, w_out, history, kv_pool
):
    num_steps, num_seqs = tokens.shape
    row_count = num_steps * num_seqs
    page_devices = lax.axis_size("pages")
    page_index = lax.axis_index("pages")
    local_heads = KV_HEADS // lax.axis_size("kv")
    kv_width = local_heads * HEAD_DIM
    inv_root = 1.0 / jnp.sqrt(jnp.float32(HEAD_DIM))
    vocab_local = embedding.shape[0]
    local_ids = tokens.reshape(-1) - lax.axis_index("kv") * vocab_local
    inside = (local_ids >= 0) & (local_ids < vocab_local)
    picked = jnp.take(embedding, jnp.clip(local_ids, 0, vocab_local - 1), axis=0)
    found = jnp.where(inside[:, None], picked, jnp.zeros_like(picked))
    embedded = lax.psum(found, "kv")
    widened = embedded.astype(jnp.float32)
    squares = jnp.sum(widened * widened, axis=1)
    normed = (widened * norm_gain.astype(jnp.float32)).astype(jnp.bfloat16)
    partial_value = jnp.dot(normed, w_qkv, preferred_element_type=jnp.float32)
    qkv_cols = partial_value.shape[1]
    packed = jnp.concatenate(
        [partial_value, squares[:, None], jnp.zeros((row_count, 127), jnp.float32)], axis=1
    )
    reduced = reduce_rows(packed, "pages")
    rows_per = row_count // page_devices
    my_rows = page_index * rows_per + jnp.arange(rows_per, dtype=jnp.int32)
    mine = finish_rows(
        reduced[:, :qkv_cols], reduced[:, qkv_cols], my_rows, prompt_len, num_seqs, local_heads
    )
    projected = lax.all_gather(
        mine.reshape(rows_per, qkv_cols), "pages", axis=0, tiled=True
    ).reshape(row_count, local_heads, PER_KV + 2, HEAD_DIM)
    queries = projected[:, :, :PER_KV]
    fresh_kv = jnp.stack([projected[:, :, PER_KV], projected[:, :, PER_KV + 1]]).reshape(
        2, num_steps, num_seqs, kv_width
    )
    buffer = jnp.concatenate(
        [history, jnp.zeros((2, num_seqs, num_steps, kv_width), jnp.bfloat16)], axis=2
    )
    snapshots = []
    for step_index in range(num_steps):
        buffer = jnp.take(buffer, parents[step_index], axis=1)
        buffer = buffer.at[:, :, PRIOR + step_index].set(fresh_kv[:, step_index])
        snapshots.append(buffer)
    stacked = jnp.stack(snapshots)
    tail_keys = stacked[:, 0].reshape(num_steps, num_seqs, HISTORY, local_heads, HEAD_DIM)
    tail_vals = stacked[:, 1].reshape(num_steps, num_seqs, HISTORY, local_heads, HEAD_DIM)
    step_query = queries.reshape(num_steps, num_seqs, local_heads, PER_KV, HEAD_DIM)
    tail_len = PRIOR + 1 + jnp.arange(num_steps, dtype=jnp.int32)
    tail_valid = (jnp.arange(HISTORY, dtype=jnp.int32)[None, :] < tail_len[:, None])[
        :, None, None, None, :
    ]
    tail_scores = (
        jnp.einsum("tbkhd,tblkd->tbkhl", step_query, tail_keys, preferred_element_type=jnp.float32)
        * inv_root
    )
    tail_scores = jnp.where(tail_valid, tail_scores, NEGATIVE)
    tail_peak = jnp.max(tail_scores, axis=-1)
    tail_exp = jnp.where(tail_valid, jnp.exp(tail_scores - tail_peak[..., None]), 0.0)
    tail_total = jnp.sum(tail_exp, axis=-1)
    tail_acc = jnp.einsum(
        "tbkhl,tblkd->tbkhd",
        tail_exp.astype(jnp.bfloat16),
        tail_vals,
        preferred_element_type=jnp.float32,
    )
    tail_part = (tail_peak.reshape(-1), tail_total.reshape(-1), tail_acc.reshape(-1, HEAD_DIM))
    slot_rows = kv_pool.shape[1]
    slot_ids = page_index * slot_rows + jnp.arange(slot_rows, dtype=jnp.int32)
    matches = page_table[:, :, None] == slot_ids[None, None, :]
    slot_used = jnp.any(matches, axis=(0, 1))
    owner_group = jnp.sum(
        jnp.where(matches, jnp.arange(GROUPS, dtype=jnp.int32)[:, None, None], 0), axis=(0, 1)
    )
    page_number = jnp.sum(
        jnp.where(matches, jnp.arange(MAX_PAGES, dtype=jnp.int32)[None, :, None], 0), axis=(0, 1)
    )
    length = jnp.take(prompt_len, owner_group)
    live_tok = slot_used[:, None] & (
        page_number[:, None] * PAGE + jnp.arange(PAGE, dtype=jnp.int32)[None, :] < length[:, None]
    )
    live_full = live_tok[None, :, None, :]
    grouped = queries.reshape(num_steps, GROUPS, BEAMS, local_heads, PER_KV, HEAD_DIM)
    chosen = jnp.take(grouped, owner_group, axis=1)
    query_rows = num_steps * BEAMS * PER_KV
    chosen = jnp.transpose(chosen, (3, 1, 0, 2, 4, 5)).reshape(
        local_heads, slot_rows, query_rows, HEAD_DIM
    )
    page_keys = jnp.transpose(
        kv_pool[0].reshape(slot_rows, PAGE, local_heads, HEAD_DIM), (2, 0, 1, 3)
    )
    page_vals = jnp.transpose(
        kv_pool[1].reshape(slot_rows, PAGE, local_heads, HEAD_DIM), (2, 0, 1, 3)
    )
    scores = (
        jnp.einsum("ksqd,kspd->ksqp", chosen, page_keys, preferred_element_type=jnp.float32)
        * inv_root
    )
    scores = jnp.where(live_full, scores, NEGATIVE)
    slot_peak = jnp.max(scores, axis=-1)
    slot_exp = jnp.where(live_full, jnp.exp(scores - slot_peak[..., None]), 0.0)
    slot_total = jnp.sum(slot_exp, axis=-1)
    slot_acc = jnp.einsum(
        "ksqp,kspd->ksqd",
        slot_exp.astype(jnp.bfloat16),
        page_vals,
        preferred_element_type=jnp.float32,
    )
    member = (owner_group[:, None] == jnp.arange(GROUPS, dtype=jnp.int32)[None, :]) & slot_used[
        :, None
    ]
    spread = jnp.where(member[None, :, :, None], slot_peak[:, :, None, :], NEGATIVE)
    group_peak = jnp.max(spread, axis=1)
    slot_base = jnp.take(group_peak, owner_group, axis=1)
    weight = jnp.where(slot_used[None, :, None], jnp.exp(slot_peak - slot_base), 0.0)
    member_f = member.astype(jnp.float32)
    group_total = jnp.einsum(
        "sg,ksq->kgq", member_f, slot_total * weight, precision=lax.Precision.HIGHEST
    )
    group_acc = jnp.einsum(
        "sg,ksqd->kgqd", member_f, slot_acc * weight[..., None], precision=lax.Precision.HIGHEST
    )
    order_small = (2, 1, 3, 0, 4)
    peak_rows = jnp.transpose(
        group_peak.reshape(local_heads, GROUPS, num_steps, BEAMS, PER_KV), order_small
    )
    total_rows = jnp.transpose(
        group_total.reshape(local_heads, GROUPS, num_steps, BEAMS, PER_KV), order_small
    )
    acc_rows = jnp.transpose(
        group_acc.reshape(local_heads, GROUPS, num_steps, BEAMS, PER_KV, HEAD_DIM),
        (2, 1, 3, 0, 4, 5),
    )
    local_part = (peak_rows.reshape(-1), total_rows.reshape(-1), acc_rows.reshape(-1, HEAD_DIM))
    with_tail = combine(local_part, tail_part)
    first = page_index == 0
    part = jax.tree.map(lambda a, b: jnp.where(first, a, b), with_tail, local_part)
    attn_rows = part[0].shape[0]
    share = attn_rows // page_devices
    stats = jnp.zeros((page_devices, 2, HEAD_DIM), jnp.float32)
    stats = stats.at[:, 0, :share].set(part[0].reshape(page_devices, share))
    stats = stats.at[:, 1, :share].set(part[1].reshape(page_devices, share))
    sent = jnp.concatenate([part[2].reshape(page_devices, share, HEAD_DIM), stats], axis=1)
    received = lax.all_to_all(sent, "pages", 0, 0, tiled=False)
    src_acc = received[:, :share]
    src_peak = received[:, share, :share]
    src_total = received[:, share + 1, :share]
    top = jnp.max(src_peak, axis=0)
    scale = jnp.exp(src_peak - top[None, :])
    total = jnp.sum(src_total * scale, axis=0)
    acc = jnp.sum(src_acc * scale[:, :, None], axis=0)
    attended_mine = (acc / total[:, None]).astype(jnp.bfloat16)
    attended = lax.all_gather(attended_mine, "pages", axis=0, tiled=True)
    flat_heads = attended.reshape(row_count, local_heads * PER_KV * HEAD_DIM)
    head_terms = jnp.dot(flat_heads, w_out, preferred_element_type=jnp.float32)
    mixed_out = lax.psum(head_terms, "kv") + widened
    return (mixed_out.astype(jnp.bfloat16).reshape(num_steps, num_seqs, -1), buffer)


def solution(mesh):
    placed = (
        P(),
        P(),
        P(),
        P(),
        P("kv", "pages"),
        P("pages"),
        P("pages", "kv"),
        P("kv", "pages"),
        P(None, None, None, "kv"),
        P(None, "pages", None, "kv"),
    )
    return jax.shard_map(
        per_device,
        mesh=mesh,
        in_specs=placed,
        out_specs=(P(None, None, "pages"), P(None, None, None, "kv")),
        check_vma=False,
    )
```

```python
import jax
import jax.numpy as jnp
from jax import lax
from jax.sharding import PartitionSpec as P

D = 7168
KV_HEADS = 8
HEAD_DIM = 128
GROUPS = 8
BEAMS = 8
PRIOR = 13
PAGE = 128
PER_KV = 7
HISTORY = 15
MAX_PAGES = 64


THETA = 5000000.0
EPSILON = 1e-05
NEGATIVE = -1e30


def rotate(values, positions):
    half_dim = HEAD_DIM // 2
    frequency = THETA ** (-(2.0 * jnp.arange(half_dim, dtype=jnp.float32)) / HEAD_DIM)
    angles = positions.astype(jnp.float32)[:, None] * frequency[None, :]
    cosine = jnp.cos(angles)[:, None, None, :]
    sine_part = jnp.sin(angles)[:, None, None, :]
    lower_part = values[..., :half_dim]
    upper_part = values[..., half_dim:]
    return jnp.concatenate(
        [
            lower_part * cosine - upper_part * sine_part,
            upper_part * cosine + lower_part * sine_part,
        ],
        axis=-1,
    )


def finish_rows(summed, norm_sums, row_ids, prompt_len, num_seqs, local_heads):
    inverse_rms = lax.rsqrt(norm_sums / D + EPSILON)
    projected = (summed * inverse_rms[:, None]).reshape(-1, local_heads, PER_KV + 2, HEAD_DIM)
    positions = jnp.take(prompt_len, row_ids % num_seqs // BEAMS) + PRIOR + row_ids // num_seqs
    turned = rotate(projected[:, :, : PER_KV + 1], positions)
    return jnp.concatenate([turned, projected[:, :, PER_KV + 1 :]], axis=2).astype(jnp.bfloat16)


def combine(earlier, later):
    peak = jnp.maximum(earlier[0], later[0])
    weight_one = jnp.exp(earlier[0] - peak)
    weight_two = jnp.exp(later[0] - peak)
    return (
        peak,
        earlier[1] * weight_one + later[1] * weight_two,
        earlier[2] * weight_one[:, None] + later[2] * weight_two[:, None],
    )


def gather_all(part, axis):
    count = lax.axis_size(axis)
    spread = jnp.broadcast_to(part[None], (count, *part.shape))
    return lax.all_to_all(spread, axis, 0, 0, tiled=False)


def reduce_rows(packed, axis):
    sources = lax.axis_size(axis)
    split = packed.reshape(sources, packed.shape[0] // sources, *packed.shape[1:])
    return jnp.sum(lax.all_to_all(split, axis, 0, 0, tiled=False), axis=0)


def per_device(
    tokens, prompt_len, page_table, parents, embedding, norm_gain, w_qkv, w_out, history, kv_pool
):
    num_steps, num_seqs = tokens.shape
    row_count = num_steps * num_seqs
    page_devices = lax.axis_size("pages")
    page_index = lax.axis_index("pages")
    local_heads = KV_HEADS // lax.axis_size("kv")
    kv_width = local_heads * HEAD_DIM
    inv_root = 1.0 / jnp.sqrt(jnp.float32(HEAD_DIM))
    vocab_local = embedding.shape[0]
    local_ids = tokens.reshape(-1) - lax.axis_index("kv") * vocab_local
    inside = (local_ids >= 0) & (local_ids < vocab_local)
    picked = jnp.take(embedding, jnp.clip(local_ids, 0, vocab_local - 1), axis=0)
    found = jnp.where(inside[:, None], picked, jnp.zeros_like(picked))
    widened = jnp.sum(gather_all(found, "kv").astype(jnp.float32), axis=0)
    squares = jnp.sum(widened * widened, axis=1)
    normed = (widened * norm_gain.astype(jnp.float32)).astype(jnp.bfloat16)
    partial_value = jnp.dot(normed, w_qkv, preferred_element_type=jnp.float32)
    qkv_cols = partial_value.shape[1]
    packed = jnp.concatenate(
        [partial_value, squares[:, None], jnp.zeros((row_count, 127), jnp.float32)], axis=1
    )
    reduced = reduce_rows(packed, "pages")
    rows_per = row_count // page_devices
    my_rows = page_index * rows_per + jnp.arange(rows_per, dtype=jnp.int32)
    mine = finish_rows(
        reduced[:, :qkv_cols], reduced[:, qkv_cols], my_rows, prompt_len, num_seqs, local_heads
    )
    projected = gather_all(mine.reshape(rows_per, qkv_cols), "pages").reshape(
        row_count, local_heads, PER_KV + 2, HEAD_DIM
    )
    queries = projected[:, :, :PER_KV]
    fresh_kv = jnp.stack([projected[:, :, PER_KV], projected[:, :, PER_KV + 1]]).reshape(
        2, num_steps, num_seqs, kv_width
    )
    buffer = jnp.concatenate(
        [history, jnp.zeros((2, num_seqs, num_steps, kv_width), jnp.bfloat16)], axis=2
    )
    snapshots = []
    for step_index in range(num_steps):
        buffer = jnp.take(buffer, parents[step_index], axis=1)
        buffer = buffer.at[:, :, PRIOR + step_index].set(fresh_kv[:, step_index])
        snapshots.append(buffer)
    stacked = jnp.stack(snapshots)
    tail_keys = stacked[:, 0].reshape(num_steps, num_seqs, HISTORY, local_heads, HEAD_DIM)
    tail_vals = stacked[:, 1].reshape(num_steps, num_seqs, HISTORY, local_heads, HEAD_DIM)
    step_query = queries.reshape(num_steps, num_seqs, local_heads, PER_KV, HEAD_DIM)
    tail_len = PRIOR + 1 + jnp.arange(num_steps, dtype=jnp.int32)
    tail_valid = (jnp.arange(HISTORY, dtype=jnp.int32)[None, :] < tail_len[:, None])[
        :, None, None, None, :
    ]
    tail_scores = (
        jnp.einsum("tbkhd,tblkd->tbkhl", step_query, tail_keys, preferred_element_type=jnp.float32)
        * inv_root
    )
    tail_scores = jnp.where(tail_valid, tail_scores, NEGATIVE)
    tail_peak = jnp.max(tail_scores, axis=-1)
    tail_exp = jnp.where(tail_valid, jnp.exp(tail_scores - tail_peak[..., None]), 0.0)
    tail_total = jnp.sum(tail_exp, axis=-1)
    tail_acc = jnp.einsum(
        "tbkhl,tblkd->tbkhd",
        tail_exp.astype(jnp.bfloat16),
        tail_vals,
        preferred_element_type=jnp.float32,
    )
    tail_part = (tail_peak.reshape(-1), tail_total.reshape(-1), tail_acc.reshape(-1, HEAD_DIM))
    slot_rows = kv_pool.shape[1]
    slot_ids = page_index * slot_rows + jnp.arange(slot_rows, dtype=jnp.int32)
    matches = page_table[:, :, None] == slot_ids[None, None, :]
    slot_used = jnp.any(matches, axis=(0, 1))
    owner_group = jnp.sum(
        jnp.where(matches, jnp.arange(GROUPS, dtype=jnp.int32)[:, None, None], 0), axis=(0, 1)
    )
    page_number = jnp.sum(
        jnp.where(matches, jnp.arange(MAX_PAGES, dtype=jnp.int32)[None, :, None], 0), axis=(0, 1)
    )
    length = jnp.take(prompt_len, owner_group)
    live_tok = slot_used[:, None] & (
        page_number[:, None] * PAGE + jnp.arange(PAGE, dtype=jnp.int32)[None, :] < length[:, None]
    )
    live_full = live_tok[None, :, None, :]
    grouped = queries.reshape(num_steps, GROUPS, BEAMS, local_heads, PER_KV, HEAD_DIM)
    chosen = jnp.take(grouped, owner_group, axis=1)
    query_rows = num_steps * BEAMS * PER_KV
    chosen = jnp.transpose(chosen, (3, 1, 0, 2, 4, 5)).reshape(
        local_heads, slot_rows, query_rows, HEAD_DIM
    )
    page_keys = jnp.transpose(
        kv_pool[0].reshape(slot_rows, PAGE, local_heads, HEAD_DIM), (2, 0, 1, 3)
    )
    page_vals = jnp.transpose(
        kv_pool[1].reshape(slot_rows, PAGE, local_heads, HEAD_DIM), (2, 0, 1, 3)
    )
    scores = (
        jnp.einsum("ksqd,kspd->ksqp", chosen, page_keys, preferred_element_type=jnp.float32)
        * inv_root
    )
    scores = jnp.where(live_full, scores, NEGATIVE)
    slot_peak = jnp.max(scores, axis=-1)
    slot_exp = jnp.where(live_full, jnp.exp(scores - slot_peak[..., None]), 0.0)
    slot_total = jnp.sum(slot_exp, axis=-1)
    slot_acc = jnp.einsum(
        "ksqp,kspd->ksqd",
        slot_exp.astype(jnp.bfloat16),
        page_vals,
        preferred_element_type=jnp.float32,
    )
    member = (owner_group[:, None] == jnp.arange(GROUPS, dtype=jnp.int32)[None, :]) & slot_used[
        :, None
    ]
    spread = jnp.where(member[None, :, :, None], slot_peak[:, :, None, :], NEGATIVE)
    group_peak = jnp.max(spread, axis=1)
    slot_base = jnp.take(group_peak, owner_group, axis=1)
    weight = jnp.where(slot_used[None, :, None], jnp.exp(slot_peak - slot_base), 0.0)
    member_f = member.astype(jnp.float32)
    group_total = jnp.einsum(
        "sg,ksq->kgq", member_f, slot_total * weight, precision=lax.Precision.HIGHEST
    )
    group_acc = jnp.einsum(
        "sg,ksqd->kgqd", member_f, slot_acc * weight[..., None], precision=lax.Precision.HIGHEST
    )
    order_small = (2, 1, 3, 0, 4)
    peak_rows = jnp.transpose(
        group_peak.reshape(local_heads, GROUPS, num_steps, BEAMS, PER_KV), order_small
    )
    total_rows = jnp.transpose(
        group_total.reshape(local_heads, GROUPS, num_steps, BEAMS, PER_KV), order_small
    )
    acc_rows = jnp.transpose(
        group_acc.reshape(local_heads, GROUPS, num_steps, BEAMS, PER_KV, HEAD_DIM),
        (2, 1, 3, 0, 4, 5),
    )
    local_part = (peak_rows.reshape(-1), total_rows.reshape(-1), acc_rows.reshape(-1, HEAD_DIM))
    with_tail = combine(local_part, tail_part)
    first = page_index == 0
    part = jax.tree.map(lambda a, b: jnp.where(first, a, b), with_tail, local_part)
    attn_rows = part[0].shape[0]
    share = attn_rows // page_devices
    stats = jnp.zeros((page_devices, 2, HEAD_DIM), jnp.float32)
    stats = stats.at[:, 0, :share].set(part[0].reshape(page_devices, share))
    stats = stats.at[:, 1, :share].set(part[1].reshape(page_devices, share))
    sent = jnp.concatenate([part[2].reshape(page_devices, share, HEAD_DIM), stats], axis=1)
    received = lax.all_to_all(sent, "pages", 0, 0, tiled=False)
    src_acc = received[:, :share]
    src_peak = received[:, share, :share]
    src_total = received[:, share + 1, :share]
    top = jnp.max(src_peak, axis=0)
    scale = jnp.exp(src_peak - top[None, :])
    total = jnp.sum(src_total * scale, axis=0)
    acc = jnp.sum(src_acc * scale[:, :, None], axis=0)
    attended_mine = (acc / total[:, None]).astype(jnp.bfloat16)
    attended = gather_all(attended_mine, "pages")
    flat_heads = attended.reshape(row_count, local_heads * PER_KV * HEAD_DIM)
    head_terms = jnp.dot(flat_heads, w_out, preferred_element_type=jnp.float32)
    mixed_out = jnp.sum(gather_all(head_terms, "kv"), axis=0) + widened
    return (mixed_out.astype(jnp.bfloat16).reshape(num_steps, num_seqs, -1), buffer)


def solution(mesh):
    placed = (
        P(),
        P(),
        P(),
        P(),
        P("kv", "pages"),
        P("pages"),
        P("pages", "kv"),
        P("kv", "pages"),
        P(None, None, None, "kv"),
        P(None, "pages", None, "kv"),
    )
    return jax.shard_map(
        per_device,
        mesh=mesh,
        in_specs=placed,
        out_specs=(P(None, None, "pages"), P(None, None, None, "kv")),
        check_vma=False,
    )
```

```python
import jax
import jax.numpy as jnp
from jax import lax
from jax.sharding import Mesh, PartitionSpec as P

D = 7168
KV_HEADS = 8
HEAD_DIM = 128
GROUPS = 8
BEAMS = 8
PRIOR = 13
PAGE = 128
PER_KV = 7
HISTORY = 15
MAX_PAGES = 64


THETA = 5000000.0
EPSILON = 1e-05
NEGATIVE = -1e30


def rotate(values, positions):
    half_dim = HEAD_DIM // 2
    frequency = THETA ** (-(2.0 * jnp.arange(half_dim, dtype=jnp.float32)) / HEAD_DIM)
    angles = positions.astype(jnp.float32)[:, None] * frequency[None, :]
    cosine = jnp.cos(angles)[:, None, None, :]
    sine_part = jnp.sin(angles)[:, None, None, :]
    lower_part = values[..., :half_dim]
    upper_part = values[..., half_dim:]
    return jnp.concatenate(
        [
            lower_part * cosine - upper_part * sine_part,
            upper_part * cosine + lower_part * sine_part,
        ],
        axis=-1,
    )


def finish_rows(summed, norm_sums, row_ids, prompt_len, num_seqs, local_heads):
    inverse_rms = lax.rsqrt(norm_sums / D + EPSILON)
    projected = (summed * inverse_rms[:, None]).reshape(-1, local_heads, PER_KV + 2, HEAD_DIM)
    positions = jnp.take(prompt_len, row_ids % num_seqs // BEAMS) + PRIOR + row_ids // num_seqs
    turned = rotate(projected[:, :, : PER_KV + 1], positions)
    return jnp.concatenate([turned, projected[:, :, PER_KV + 1 :]], axis=2).astype(jnp.bfloat16)


def combine(earlier, later):
    peak = jnp.maximum(earlier[0], later[0])
    weight_one = jnp.exp(earlier[0] - peak)
    weight_two = jnp.exp(later[0] - peak)
    return (
        peak,
        earlier[1] * weight_one + later[1] * weight_two,
        earlier[2] * weight_one[:, None] + later[2] * weight_two[:, None],
    )


def gather_all(part, axis):
    count = lax.axis_size(axis)
    spread = jnp.broadcast_to(part[None], (count, *part.shape))
    return lax.all_to_all(spread, axis, 0, 0, tiled=False)


def gather_rows(part):
    inner = gather_all(part, "pz")
    inner = inner.reshape(-1, *part.shape[1:])
    outer = gather_all(inner, "px")
    return outer.reshape(-1, *part.shape[1:])


def reduce_rows(packed):
    for axis in ("px", "pz"):
        sources = lax.axis_size(axis)
        split = packed.reshape(sources, packed.shape[0] // sources, *packed.shape[1:])
        packed = jnp.sum(lax.all_to_all(split, axis, 0, 0, tiled=False), axis=0)
    return packed


def merge_blocks(received, share):
    peak = received[:, ..., share, :share]
    top = jnp.max(peak, axis=0)
    scale = jnp.exp(peak - top[None])
    total = jnp.sum(received[:, ..., share + 1, :share] * scale, axis=0)
    acc = jnp.sum(received[:, ..., :share, :] * scale[..., None], axis=0)
    return top, total, acc


def pack_blocks(top, total, acc, share):
    stats = jnp.zeros((*acc.shape[:-2], 2, HEAD_DIM), jnp.float32)
    stats = stats.at[..., 0, :share].set(top)
    stats = stats.at[..., 1, :share].set(total)
    return jnp.concatenate([acc, stats], axis=-2)


def per_device(
    tokens, prompt_len, page_table, parents, embedding, norm_gain, w_qkv, w_out, history, kv_pool
):
    num_steps, num_seqs = tokens.shape
    row_count = num_steps * num_seqs
    outer_count = lax.axis_size("px")
    inner_count = lax.axis_size("pz")
    page_devices = outer_count * inner_count
    page_index = lax.axis_index("px") * inner_count + lax.axis_index("pz")
    local_heads = KV_HEADS // lax.axis_size("kv")
    kv_width = local_heads * HEAD_DIM
    inv_root = 1.0 / jnp.sqrt(jnp.float32(HEAD_DIM))
    vocab_local = embedding.shape[0]
    local_ids = tokens.reshape(-1) - lax.axis_index("kv") * vocab_local
    inside = (local_ids >= 0) & (local_ids < vocab_local)
    picked = jnp.take(embedding, jnp.clip(local_ids, 0, vocab_local - 1), axis=0)
    found = jnp.where(inside[:, None], picked, jnp.zeros_like(picked))
    widened = jnp.sum(gather_all(found, "kv").astype(jnp.float32), axis=0)
    squares = jnp.sum(widened * widened, axis=1)
    normed = (widened * norm_gain.astype(jnp.float32)).astype(jnp.bfloat16)
    partial_value = jnp.dot(normed, w_qkv, preferred_element_type=jnp.float32)
    qkv_cols = partial_value.shape[1]
    packed = jnp.concatenate(
        [partial_value, squares[:, None], jnp.zeros((row_count, 127), jnp.float32)], axis=1
    )
    reduced = reduce_rows(packed)
    rows_per = row_count // page_devices
    my_rows = page_index * rows_per + jnp.arange(rows_per, dtype=jnp.int32)
    mine = finish_rows(
        reduced[:, :qkv_cols], reduced[:, qkv_cols], my_rows, prompt_len, num_seqs, local_heads
    )
    projected = gather_rows(mine.reshape(rows_per, qkv_cols)).reshape(
        row_count, local_heads, PER_KV + 2, HEAD_DIM
    )
    queries = projected[:, :, :PER_KV]
    fresh_kv = jnp.stack([projected[:, :, PER_KV], projected[:, :, PER_KV + 1]]).reshape(
        2, num_steps, num_seqs, kv_width
    )
    buffer = jnp.concatenate(
        [history, jnp.zeros((2, num_seqs, num_steps, kv_width), jnp.bfloat16)], axis=2
    )
    snapshots = []
    for step_index in range(num_steps):
        buffer = jnp.take(buffer, parents[step_index], axis=1)
        buffer = buffer.at[:, :, PRIOR + step_index].set(fresh_kv[:, step_index])
        snapshots.append(buffer)
    stacked = jnp.stack(snapshots)
    tail_keys = stacked[:, 0].reshape(num_steps, num_seqs, HISTORY, local_heads, HEAD_DIM)
    tail_vals = stacked[:, 1].reshape(num_steps, num_seqs, HISTORY, local_heads, HEAD_DIM)
    step_query = queries.reshape(num_steps, num_seqs, local_heads, PER_KV, HEAD_DIM)
    tail_len = PRIOR + 1 + jnp.arange(num_steps, dtype=jnp.int32)
    tail_valid = (jnp.arange(HISTORY, dtype=jnp.int32)[None, :] < tail_len[:, None])[
        :, None, None, None, :
    ]
    tail_scores = (
        jnp.einsum("tbkhd,tblkd->tbkhl", step_query, tail_keys, preferred_element_type=jnp.float32)
        * inv_root
    )
    tail_scores = jnp.where(tail_valid, tail_scores, NEGATIVE)
    tail_peak = jnp.max(tail_scores, axis=-1)
    tail_exp = jnp.where(tail_valid, jnp.exp(tail_scores - tail_peak[..., None]), 0.0)
    tail_total = jnp.sum(tail_exp, axis=-1)
    tail_acc = jnp.einsum(
        "tbkhl,tblkd->tbkhd",
        tail_exp.astype(jnp.bfloat16),
        tail_vals,
        preferred_element_type=jnp.float32,
    )
    tail_part = (tail_peak.reshape(-1), tail_total.reshape(-1), tail_acc.reshape(-1, HEAD_DIM))
    slot_rows = kv_pool.shape[1]
    slot_ids = page_index * slot_rows + jnp.arange(slot_rows, dtype=jnp.int32)
    matches = page_table[:, :, None] == slot_ids[None, None, :]
    slot_used = jnp.any(matches, axis=(0, 1))
    owner_group = jnp.sum(
        jnp.where(matches, jnp.arange(GROUPS, dtype=jnp.int32)[:, None, None], 0), axis=(0, 1)
    )
    page_number = jnp.sum(
        jnp.where(matches, jnp.arange(MAX_PAGES, dtype=jnp.int32)[None, :, None], 0), axis=(0, 1)
    )
    length = jnp.take(prompt_len, owner_group)
    live_tok = slot_used[:, None] & (
        page_number[:, None] * PAGE + jnp.arange(PAGE, dtype=jnp.int32)[None, :] < length[:, None]
    )
    live_full = live_tok[None, :, None, :]
    grouped = queries.reshape(num_steps, GROUPS, BEAMS, local_heads, PER_KV, HEAD_DIM)
    chosen = jnp.take(grouped, owner_group, axis=1)
    query_rows = num_steps * BEAMS * PER_KV
    chosen = jnp.transpose(chosen, (3, 1, 0, 2, 4, 5)).reshape(
        local_heads, slot_rows, query_rows, HEAD_DIM
    )
    page_keys = jnp.transpose(
        kv_pool[0].reshape(slot_rows, PAGE, local_heads, HEAD_DIM), (2, 0, 1, 3)
    )
    page_vals = jnp.transpose(
        kv_pool[1].reshape(slot_rows, PAGE, local_heads, HEAD_DIM), (2, 0, 1, 3)
    )
    scores = (
        jnp.einsum("ksqd,kspd->ksqp", chosen, page_keys, preferred_element_type=jnp.float32)
        * inv_root
    )
    scores = jnp.where(live_full, scores, NEGATIVE)
    slot_peak = jnp.max(scores, axis=-1)
    slot_exp = jnp.where(live_full, jnp.exp(scores - slot_peak[..., None]), 0.0)
    slot_total = jnp.sum(slot_exp, axis=-1)
    slot_acc = jnp.einsum(
        "ksqp,kspd->ksqd",
        slot_exp.astype(jnp.bfloat16),
        page_vals,
        preferred_element_type=jnp.float32,
    )
    member = (owner_group[:, None] == jnp.arange(GROUPS, dtype=jnp.int32)[None, :]) & slot_used[
        :, None
    ]
    spread = jnp.where(member[None, :, :, None], slot_peak[:, :, None, :], NEGATIVE)
    group_peak = jnp.max(spread, axis=1)
    slot_base = jnp.take(group_peak, owner_group, axis=1)
    weight = jnp.where(slot_used[None, :, None], jnp.exp(slot_peak - slot_base), 0.0)
    member_f = member.astype(jnp.float32)
    group_total = jnp.einsum(
        "sg,ksq->kgq", member_f, slot_total * weight, precision=lax.Precision.HIGHEST
    )
    group_acc = jnp.einsum(
        "sg,ksqd->kgqd", member_f, slot_acc * weight[..., None], precision=lax.Precision.HIGHEST
    )
    order_small = (2, 1, 3, 0, 4)
    peak_rows = jnp.transpose(
        group_peak.reshape(local_heads, GROUPS, num_steps, BEAMS, PER_KV), order_small
    )
    total_rows = jnp.transpose(
        group_total.reshape(local_heads, GROUPS, num_steps, BEAMS, PER_KV), order_small
    )
    acc_rows = jnp.transpose(
        group_acc.reshape(local_heads, GROUPS, num_steps, BEAMS, PER_KV, HEAD_DIM),
        (2, 1, 3, 0, 4, 5),
    )
    local_part = (peak_rows.reshape(-1), total_rows.reshape(-1), acc_rows.reshape(-1, HEAD_DIM))
    with_tail = combine(local_part, tail_part)
    first = page_index == 0
    part = jax.tree.map(lambda a, b: jnp.where(first, a, b), with_tail, local_part)
    attn_rows = part[0].shape[0]
    share = attn_rows // page_devices
    sent = pack_blocks(
        part[0].reshape(outer_count, inner_count, share),
        part[1].reshape(outer_count, inner_count, share),
        part[2].reshape(outer_count, inner_count, share, HEAD_DIM),
        share,
    )
    stage = merge_blocks(lax.all_to_all(sent, "px", 0, 0, tiled=False), share)
    sent = pack_blocks(*stage, share)
    top, total, acc = merge_blocks(lax.all_to_all(sent, "pz", 0, 0, tiled=False), share)
    attended_mine = (acc / total[:, None]).astype(jnp.bfloat16)
    attended = gather_rows(attended_mine)
    flat_heads = attended.reshape(row_count, local_heads * PER_KV * HEAD_DIM)
    head_terms = jnp.dot(flat_heads, w_out, preferred_element_type=jnp.float32)
    mixed_out = jnp.sum(gather_all(head_terms, "kv"), axis=0) + widened
    return (mixed_out.astype(jnp.bfloat16).reshape(num_steps, num_seqs, -1), buffer)


def solution(mesh):
    row = mesh.devices[0]
    outer = len({device.coords[0] for device in row})
    split = Mesh(
        mesh.devices.reshape(mesh.devices.shape[0], outer, row.size // outer), ("kv", "px", "pz")
    )
    pages = ("px", "pz")
    placed = (
        P(),
        P(),
        P(),
        P(),
        P("kv", pages),
        P(pages),
        P(pages, "kv"),
        P("kv", pages),
        P(None, None, None, "kv"),
        P(None, pages, None, "kv"),
    )
    return jax.shard_map(
        per_device,
        mesh=split,
        in_specs=placed,
        out_specs=(P(None, None, pages), P(None, None, None, "kv")),
        check_vma=False,
    )
```

```python
import jax
import jax.numpy as jnp
from jax import lax
from jax.sharding import Mesh, PartitionSpec as P

D = 7168
KV_HEADS = 8
HEAD_DIM = 128
GROUPS = 8
BEAMS = 8
PRIOR = 13
PAGE = 128
PER_KV = 7
HISTORY = 15
MAX_PAGES = 64


THETA = 5000000.0
EPSILON = 1e-05
NEGATIVE = -1e30
STAGES = ("px", "pzh", "pzl")


def rotate(values, positions):
    half_dim = HEAD_DIM // 2
    frequency = THETA ** (-(2.0 * jnp.arange(half_dim, dtype=jnp.float32)) / HEAD_DIM)
    angles = positions.astype(jnp.float32)[:, None] * frequency[None, :]
    cosine = jnp.cos(angles)[:, None, None, :]
    sine_part = jnp.sin(angles)[:, None, None, :]
    lower_part = values[..., :half_dim]
    upper_part = values[..., half_dim:]
    return jnp.concatenate(
        [
            lower_part * cosine - upper_part * sine_part,
            upper_part * cosine + lower_part * sine_part,
        ],
        axis=-1,
    )


def finish_rows(summed, norm_sums, row_ids, prompt_len, num_seqs, local_heads):
    inverse_rms = lax.rsqrt(norm_sums / D + EPSILON)
    projected = (summed * inverse_rms[:, None]).reshape(-1, local_heads, PER_KV + 2, HEAD_DIM)
    positions = jnp.take(prompt_len, row_ids % num_seqs // BEAMS) + PRIOR + row_ids // num_seqs
    turned = rotate(projected[:, :, : PER_KV + 1], positions)
    return jnp.concatenate([turned, projected[:, :, PER_KV + 1 :]], axis=2).astype(jnp.bfloat16)


def combine(earlier, later):
    peak = jnp.maximum(earlier[0], later[0])
    weight_one = jnp.exp(earlier[0] - peak)
    weight_two = jnp.exp(later[0] - peak)
    return (
        peak,
        earlier[1] * weight_one + later[1] * weight_two,
        earlier[2] * weight_one[:, None] + later[2] * weight_two[:, None],
    )


def gather_all(part, axis):
    count = lax.axis_size(axis)
    spread = jnp.broadcast_to(part[None], (count, *part.shape))
    return lax.all_to_all(spread, axis, 0, 0, tiled=False)


def gather_rows(part):
    for axis in reversed(STAGES):
        part = gather_all(part, axis).reshape(-1, *part.shape[1:])
    return part


def reduce_rows(packed):
    for axis in STAGES:
        sources = lax.axis_size(axis)
        split = packed.reshape(sources, packed.shape[0] // sources, *packed.shape[1:])
        packed = jnp.sum(lax.all_to_all(split, axis, 0, 0, tiled=False), axis=0)
    return packed


def merge_blocks(received, share):
    peak = received[:, ..., share, :share]
    top = jnp.max(peak, axis=0)
    scale = jnp.exp(peak - top[None])
    total = jnp.sum(received[:, ..., share + 1, :share] * scale, axis=0)
    acc = jnp.sum(received[:, ..., :share, :] * scale[..., None], axis=0)
    return top, total, acc


def pack_blocks(top, total, acc, share):
    stats = jnp.zeros((*acc.shape[:-2], 2, HEAD_DIM), jnp.float32)
    stats = stats.at[..., 0, :share].set(top)
    stats = stats.at[..., 1, :share].set(total)
    return jnp.concatenate([acc, stats], axis=-2)


def per_device(
    tokens, prompt_len, page_table, parents, embedding, norm_gain, w_qkv, w_out, history, kv_pool
):
    num_steps, num_seqs = tokens.shape
    row_count = num_steps * num_seqs
    stage_sizes = tuple(lax.axis_size(axis) for axis in STAGES)
    page_devices = 1
    page_index = 0
    for axis, size in zip(STAGES, stage_sizes):
        page_devices = page_devices * size
        page_index = page_index * size + lax.axis_index(axis)
    local_heads = KV_HEADS // lax.axis_size("kv")
    kv_width = local_heads * HEAD_DIM
    inv_root = 1.0 / jnp.sqrt(jnp.float32(HEAD_DIM))
    vocab_local = embedding.shape[0]
    local_ids = tokens.reshape(-1) - lax.axis_index("kv") * vocab_local
    inside = (local_ids >= 0) & (local_ids < vocab_local)
    picked = jnp.take(embedding, jnp.clip(local_ids, 0, vocab_local - 1), axis=0)
    found = jnp.where(inside[:, None], picked, jnp.zeros_like(picked))
    widened = jnp.sum(gather_all(found, "kv").astype(jnp.float32), axis=0)
    squares = jnp.sum(widened * widened, axis=1)
    normed = (widened * norm_gain.astype(jnp.float32)).astype(jnp.bfloat16)
    partial_value = jnp.dot(normed, w_qkv, preferred_element_type=jnp.float32)
    qkv_cols = partial_value.shape[1]
    packed = jnp.concatenate(
        [partial_value, squares[:, None], jnp.zeros((row_count, 127), jnp.float32)], axis=1
    )
    reduced = reduce_rows(packed)
    rows_per = row_count // page_devices
    my_rows = page_index * rows_per + jnp.arange(rows_per, dtype=jnp.int32)
    mine = finish_rows(
        reduced[:, :qkv_cols], reduced[:, qkv_cols], my_rows, prompt_len, num_seqs, local_heads
    )
    projected = gather_rows(mine.reshape(rows_per, qkv_cols)).reshape(
        row_count, local_heads, PER_KV + 2, HEAD_DIM
    )
    queries = projected[:, :, :PER_KV]
    fresh_kv = jnp.stack([projected[:, :, PER_KV], projected[:, :, PER_KV + 1]]).reshape(
        2, num_steps, num_seqs, kv_width
    )
    buffer = jnp.concatenate(
        [history, jnp.zeros((2, num_seqs, num_steps, kv_width), jnp.bfloat16)], axis=2
    )
    snapshots = []
    for step_index in range(num_steps):
        buffer = jnp.take(buffer, parents[step_index], axis=1)
        buffer = buffer.at[:, :, PRIOR + step_index].set(fresh_kv[:, step_index])
        snapshots.append(buffer)
    stacked = jnp.stack(snapshots)
    tail_keys = stacked[:, 0].reshape(num_steps, num_seqs, HISTORY, local_heads, HEAD_DIM)
    tail_vals = stacked[:, 1].reshape(num_steps, num_seqs, HISTORY, local_heads, HEAD_DIM)
    step_query = queries.reshape(num_steps, num_seqs, local_heads, PER_KV, HEAD_DIM)
    tail_len = PRIOR + 1 + jnp.arange(num_steps, dtype=jnp.int32)
    tail_valid = (jnp.arange(HISTORY, dtype=jnp.int32)[None, :] < tail_len[:, None])[
        :, None, None, None, :
    ]
    tail_scores = (
        jnp.einsum("tbkhd,tblkd->tbkhl", step_query, tail_keys, preferred_element_type=jnp.float32)
        * inv_root
    )
    tail_scores = jnp.where(tail_valid, tail_scores, NEGATIVE)
    tail_peak = jnp.max(tail_scores, axis=-1)
    tail_exp = jnp.where(tail_valid, jnp.exp(tail_scores - tail_peak[..., None]), 0.0)
    tail_total = jnp.sum(tail_exp, axis=-1)
    tail_acc = jnp.einsum(
        "tbkhl,tblkd->tbkhd",
        tail_exp.astype(jnp.bfloat16),
        tail_vals,
        preferred_element_type=jnp.float32,
    )
    tail_part = (tail_peak.reshape(-1), tail_total.reshape(-1), tail_acc.reshape(-1, HEAD_DIM))
    slot_rows = kv_pool.shape[1]
    slot_ids = page_index * slot_rows + jnp.arange(slot_rows, dtype=jnp.int32)
    matches = page_table[:, :, None] == slot_ids[None, None, :]
    slot_used = jnp.any(matches, axis=(0, 1))
    owner_group = jnp.sum(
        jnp.where(matches, jnp.arange(GROUPS, dtype=jnp.int32)[:, None, None], 0), axis=(0, 1)
    )
    page_number = jnp.sum(
        jnp.where(matches, jnp.arange(MAX_PAGES, dtype=jnp.int32)[None, :, None], 0), axis=(0, 1)
    )
    length = jnp.take(prompt_len, owner_group)
    live_tok = slot_used[:, None] & (
        page_number[:, None] * PAGE + jnp.arange(PAGE, dtype=jnp.int32)[None, :] < length[:, None]
    )
    live_full = live_tok[None, :, None, :]
    grouped = queries.reshape(num_steps, GROUPS, BEAMS, local_heads, PER_KV, HEAD_DIM)
    chosen = jnp.take(grouped, owner_group, axis=1)
    query_rows = num_steps * BEAMS * PER_KV
    chosen = jnp.transpose(chosen, (3, 1, 0, 2, 4, 5)).reshape(
        local_heads, slot_rows, query_rows, HEAD_DIM
    )
    page_keys = jnp.transpose(
        kv_pool[0].reshape(slot_rows, PAGE, local_heads, HEAD_DIM), (2, 0, 1, 3)
    )
    page_vals = jnp.transpose(
        kv_pool[1].reshape(slot_rows, PAGE, local_heads, HEAD_DIM), (2, 0, 1, 3)
    )
    scores = (
        jnp.einsum("ksqd,kspd->ksqp", chosen, page_keys, preferred_element_type=jnp.float32)
        * inv_root
    )
    scores = jnp.where(live_full, scores, NEGATIVE)
    slot_peak = jnp.max(scores, axis=-1)
    slot_exp = jnp.where(live_full, jnp.exp(scores - slot_peak[..., None]), 0.0)
    slot_total = jnp.sum(slot_exp, axis=-1)
    slot_acc = jnp.einsum(
        "ksqp,kspd->ksqd",
        slot_exp.astype(jnp.bfloat16),
        page_vals,
        preferred_element_type=jnp.float32,
    )
    member = (owner_group[:, None] == jnp.arange(GROUPS, dtype=jnp.int32)[None, :]) & slot_used[
        :, None
    ]
    spread = jnp.where(member[None, :, :, None], slot_peak[:, :, None, :], NEGATIVE)
    group_peak = jnp.max(spread, axis=1)
    slot_base = jnp.take(group_peak, owner_group, axis=1)
    weight = jnp.where(slot_used[None, :, None], jnp.exp(slot_peak - slot_base), 0.0)
    member_f = member.astype(jnp.float32)
    group_total = jnp.einsum(
        "sg,ksq->kgq", member_f, slot_total * weight, precision=lax.Precision.HIGHEST
    )
    group_acc = jnp.einsum(
        "sg,ksqd->kgqd", member_f, slot_acc * weight[..., None], precision=lax.Precision.HIGHEST
    )
    order_small = (2, 1, 3, 0, 4)
    peak_rows = jnp.transpose(
        group_peak.reshape(local_heads, GROUPS, num_steps, BEAMS, PER_KV), order_small
    )
    total_rows = jnp.transpose(
        group_total.reshape(local_heads, GROUPS, num_steps, BEAMS, PER_KV), order_small
    )
    acc_rows = jnp.transpose(
        group_acc.reshape(local_heads, GROUPS, num_steps, BEAMS, PER_KV, HEAD_DIM),
        (2, 1, 3, 0, 4, 5),
    )
    local_part = (peak_rows.reshape(-1), total_rows.reshape(-1), acc_rows.reshape(-1, HEAD_DIM))
    with_tail = combine(local_part, tail_part)
    first = page_index == 0
    part = jax.tree.map(lambda a, b: jnp.where(first, a, b), with_tail, local_part)
    attn_rows = part[0].shape[0]
    share = attn_rows // page_devices
    sent = pack_blocks(
        part[0].reshape(*stage_sizes, share),
        part[1].reshape(*stage_sizes, share),
        part[2].reshape(*stage_sizes, share, HEAD_DIM),
        share,
    )
    for axis in STAGES:
        stage = merge_blocks(lax.all_to_all(sent, axis, 0, 0, tiled=False), share)
        sent = pack_blocks(*stage, share)
    top, total, acc = stage
    attended_mine = (acc / total[:, None]).astype(jnp.bfloat16)
    attended = gather_rows(attended_mine)
    flat_heads = attended.reshape(row_count, local_heads * PER_KV * HEAD_DIM)
    head_terms = jnp.dot(flat_heads, w_out, preferred_element_type=jnp.float32)
    mixed_out = jnp.sum(gather_all(head_terms, "kv"), axis=0) + widened
    return (mixed_out.astype(jnp.bfloat16).reshape(num_steps, num_seqs, -1), buffer)


def solution(mesh):
    row = mesh.devices[0]
    outer = len({device.coords[0] for device in row})
    inner = row.size // outer
    low = 4 if inner % 4 == 0 else inner
    split = Mesh(
        mesh.devices.reshape(mesh.devices.shape[0], outer, inner // low, low),
        ("kv",) + STAGES,
    )
    pages = STAGES
    placed = (
        P(),
        P(),
        P(),
        P(),
        P("kv", pages),
        P(pages),
        P(pages, "kv"),
        P("kv", pages),
        P(None, None, None, "kv"),
        P(None, pages, None, "kv"),
    )
    return jax.shard_map(
        per_device,
        mesh=split,
        in_specs=placed,
        out_specs=(P(None, None, pages), P(None, None, None, "kv")),
        check_vma=False,
    )
```

```python
import jax
import jax.numpy as jnp
from jax import lax
from jax.sharding import Mesh, PartitionSpec as P

D = 7168
KV_HEADS = 8
HEAD_DIM = 128
GROUPS = 8
BEAMS = 8
PRIOR = 13
PAGE = 128
PER_KV = 7
HISTORY = 15
MAX_PAGES = 64


THETA = 5000000.0
EPSILON = 1e-05
NEGATIVE = -1e30
STAGES = ("px", "pz")


def rotate(values, positions):
    half_dim = HEAD_DIM // 2
    frequency = THETA ** (-(2.0 * jnp.arange(half_dim, dtype=jnp.float32)) / HEAD_DIM)
    angles = positions.astype(jnp.float32)[:, None] * frequency[None, :]
    cosine = jnp.cos(angles)[:, None, None, :]
    sine_part = jnp.sin(angles)[:, None, None, :]
    lower_part = values[..., :half_dim]
    upper_part = values[..., half_dim:]
    return jnp.concatenate(
        [
            lower_part * cosine - upper_part * sine_part,
            upper_part * cosine + lower_part * sine_part,
        ],
        axis=-1,
    )


def finish_rows(summed, norm_sums, row_ids, prompt_len, num_seqs, local_heads):
    inverse_rms = lax.rsqrt(norm_sums / D + EPSILON)
    projected = (summed * inverse_rms[:, None]).reshape(-1, local_heads, PER_KV + 2, HEAD_DIM)
    positions = jnp.take(prompt_len, row_ids % num_seqs // BEAMS) + PRIOR + row_ids // num_seqs
    turned = rotate(projected[:, :, : PER_KV + 1], positions)
    return jnp.concatenate([turned, projected[:, :, PER_KV + 1 :]], axis=2).astype(jnp.bfloat16)


def combine(earlier, later):
    peak = jnp.maximum(earlier[0], later[0])
    weight_one = jnp.exp(earlier[0] - peak)
    weight_two = jnp.exp(later[0] - peak)
    return (
        peak,
        earlier[1] * weight_one + later[1] * weight_two,
        earlier[2] * weight_one[:, None] + later[2] * weight_two[:, None],
    )


def gather_all(part, axis):
    count = lax.axis_size(axis)
    spread = jnp.broadcast_to(part.reshape(1, -1), (count, part.size))
    return lax.all_to_all(spread, axis, 0, 0, tiled=False).reshape(count, *part.shape)


def gather_rows(part):
    for axis in reversed(STAGES):
        part = gather_all(part, axis).reshape(-1, *part.shape[1:])
    return part


def reduce_rows(packed):
    for axis in STAGES:
        sources = lax.axis_size(axis)
        block = (packed.shape[0] // sources, *packed.shape[1:])
        split = packed.reshape(sources, -1)
        packed = jnp.sum(lax.all_to_all(split, axis, 0, 0, tiled=False), axis=0).reshape(block)
    return packed


def merge_blocks(received, share):
    peak = received[:, ..., share, :share]
    top = jnp.max(peak, axis=0)
    scale = jnp.exp(peak - top[None])
    total = jnp.sum(received[:, ..., share + 1, :share] * scale, axis=0)
    acc = jnp.sum(received[:, ..., :share, :] * scale[..., None], axis=0)
    return top, total, acc


def pack_blocks(top, total, acc, share):
    stats = jnp.zeros((*acc.shape[:-2], 2, HEAD_DIM), jnp.float32)
    stats = stats.at[..., 0, :share].set(top)
    stats = stats.at[..., 1, :share].set(total)
    return jnp.concatenate([acc, stats], axis=-2)


def per_device(
    tokens, prompt_len, page_table, parents, embedding, norm_gain, w_qkv, w_out, history, kv_pool
):
    num_steps, num_seqs = tokens.shape
    row_count = num_steps * num_seqs
    stage_sizes = tuple(lax.axis_size(axis) for axis in STAGES)
    page_devices = 1
    page_index = 0
    for axis, size in zip(STAGES, stage_sizes):
        page_devices = page_devices * size
        page_index = page_index * size + lax.axis_index(axis)
    local_heads = KV_HEADS // lax.axis_size("kv")
    kv_width = local_heads * HEAD_DIM
    inv_root = 1.0 / jnp.sqrt(jnp.float32(HEAD_DIM))
    vocab_local = embedding.shape[0]
    local_ids = tokens.reshape(-1) - lax.axis_index("kv") * vocab_local
    inside = (local_ids >= 0) & (local_ids < vocab_local)
    picked = jnp.take(embedding, jnp.clip(local_ids, 0, vocab_local - 1), axis=0)
    found = jnp.where(inside[:, None], picked, jnp.zeros_like(picked))
    widened = jnp.sum(gather_all(found, "kv").astype(jnp.float32), axis=0)
    squares = jnp.sum(widened * widened, axis=1)
    normed = (widened * norm_gain.astype(jnp.float32)).astype(jnp.bfloat16)
    partial_value = jnp.dot(normed, w_qkv, preferred_element_type=jnp.float32)
    qkv_cols = partial_value.shape[1]
    packed = jnp.concatenate(
        [partial_value, squares[:, None], jnp.zeros((row_count, 127), jnp.float32)], axis=1
    )
    reduced = reduce_rows(packed)
    rows_per = row_count // page_devices
    my_rows = page_index * rows_per + jnp.arange(rows_per, dtype=jnp.int32)
    mine = finish_rows(
        reduced[:, :qkv_cols], reduced[:, qkv_cols], my_rows, prompt_len, num_seqs, local_heads
    )
    projected = gather_rows(mine.reshape(rows_per, qkv_cols)).reshape(
        row_count, local_heads, PER_KV + 2, HEAD_DIM
    )
    queries = projected[:, :, :PER_KV]
    fresh_kv = jnp.stack([projected[:, :, PER_KV], projected[:, :, PER_KV + 1]]).reshape(
        2, num_steps, num_seqs, kv_width
    )
    buffer = jnp.concatenate(
        [history, jnp.zeros((2, num_seqs, num_steps, kv_width), jnp.bfloat16)], axis=2
    )
    snapshots = []
    for step_index in range(num_steps):
        buffer = jnp.take(buffer, parents[step_index], axis=1)
        buffer = buffer.at[:, :, PRIOR + step_index].set(fresh_kv[:, step_index])
        snapshots.append(buffer)
    stacked = jnp.stack(snapshots)
    tail_keys = stacked[:, 0].reshape(num_steps, num_seqs, HISTORY, local_heads, HEAD_DIM)
    tail_vals = stacked[:, 1].reshape(num_steps, num_seqs, HISTORY, local_heads, HEAD_DIM)
    step_query = queries.reshape(num_steps, num_seqs, local_heads, PER_KV, HEAD_DIM)
    tail_len = PRIOR + 1 + jnp.arange(num_steps, dtype=jnp.int32)
    tail_valid = (jnp.arange(HISTORY, dtype=jnp.int32)[None, :] < tail_len[:, None])[
        :, None, None, None, :
    ]
    tail_scores = (
        jnp.einsum("tbkhd,tblkd->tbkhl", step_query, tail_keys, preferred_element_type=jnp.float32)
        * inv_root
    )
    tail_scores = jnp.where(tail_valid, tail_scores, NEGATIVE)
    tail_peak = jnp.max(tail_scores, axis=-1)
    tail_exp = jnp.where(tail_valid, jnp.exp(tail_scores - tail_peak[..., None]), 0.0)
    tail_total = jnp.sum(tail_exp, axis=-1)
    tail_acc = jnp.einsum(
        "tbkhl,tblkd->tbkhd",
        tail_exp.astype(jnp.bfloat16),
        tail_vals,
        preferred_element_type=jnp.float32,
    )
    tail_part = (tail_peak.reshape(-1), tail_total.reshape(-1), tail_acc.reshape(-1, HEAD_DIM))
    slot_rows = kv_pool.shape[1]
    slot_ids = page_index * slot_rows + jnp.arange(slot_rows, dtype=jnp.int32)
    matches = page_table[:, :, None] == slot_ids[None, None, :]
    slot_used = jnp.any(matches, axis=(0, 1))
    owner_group = jnp.sum(
        jnp.where(matches, jnp.arange(GROUPS, dtype=jnp.int32)[:, None, None], 0), axis=(0, 1)
    )
    page_number = jnp.sum(
        jnp.where(matches, jnp.arange(MAX_PAGES, dtype=jnp.int32)[None, :, None], 0), axis=(0, 1)
    )
    length = jnp.take(prompt_len, owner_group)
    live_tok = slot_used[:, None] & (
        page_number[:, None] * PAGE + jnp.arange(PAGE, dtype=jnp.int32)[None, :] < length[:, None]
    )
    live_full = live_tok[None, :, None, :]
    grouped = queries.reshape(num_steps, GROUPS, BEAMS, local_heads, PER_KV, HEAD_DIM)
    chosen = jnp.take(grouped, owner_group, axis=1)
    query_rows = num_steps * BEAMS * PER_KV
    chosen = jnp.transpose(chosen, (3, 1, 0, 2, 4, 5)).reshape(
        local_heads, slot_rows, query_rows, HEAD_DIM
    )
    page_keys = jnp.transpose(
        kv_pool[0].reshape(slot_rows, PAGE, local_heads, HEAD_DIM), (2, 0, 1, 3)
    )
    page_vals = jnp.transpose(
        kv_pool[1].reshape(slot_rows, PAGE, local_heads, HEAD_DIM), (2, 0, 1, 3)
    )
    scores = (
        jnp.einsum("ksqd,kspd->ksqp", chosen, page_keys, preferred_element_type=jnp.float32)
        * inv_root
    )
    scores = jnp.where(live_full, scores, NEGATIVE)
    slot_peak = jnp.max(scores, axis=-1)
    slot_exp = jnp.where(live_full, jnp.exp(scores - slot_peak[..., None]), 0.0)
    slot_total = jnp.sum(slot_exp, axis=-1)
    slot_acc = jnp.einsum(
        "ksqp,kspd->ksqd",
        slot_exp.astype(jnp.bfloat16),
        page_vals,
        preferred_element_type=jnp.float32,
    )
    member = (owner_group[:, None] == jnp.arange(GROUPS, dtype=jnp.int32)[None, :]) & slot_used[
        :, None
    ]
    spread = jnp.where(member[None, :, :, None], slot_peak[:, :, None, :], NEGATIVE)
    group_peak = jnp.max(spread, axis=1)
    slot_base = jnp.take(group_peak, owner_group, axis=1)
    weight = jnp.where(slot_used[None, :, None], jnp.exp(slot_peak - slot_base), 0.0)
    member_f = member.astype(jnp.float32)
    group_total = jnp.einsum(
        "sg,ksq->kgq", member_f, slot_total * weight, precision=lax.Precision.HIGHEST
    )
    group_acc = jnp.einsum(
        "sg,ksqd->kgqd", member_f, slot_acc * weight[..., None], precision=lax.Precision.HIGHEST
    )
    order_small = (2, 1, 3, 0, 4)
    peak_rows = jnp.transpose(
        group_peak.reshape(local_heads, GROUPS, num_steps, BEAMS, PER_KV), order_small
    )
    total_rows = jnp.transpose(
        group_total.reshape(local_heads, GROUPS, num_steps, BEAMS, PER_KV), order_small
    )
    acc_rows = jnp.transpose(
        group_acc.reshape(local_heads, GROUPS, num_steps, BEAMS, PER_KV, HEAD_DIM),
        (2, 1, 3, 0, 4, 5),
    )
    local_part = (peak_rows.reshape(-1), total_rows.reshape(-1), acc_rows.reshape(-1, HEAD_DIM))
    with_tail = combine(local_part, tail_part)
    first = page_index == 0
    part = jax.tree.map(lambda a, b: jnp.where(first, a, b), with_tail, local_part)
    attn_rows = part[0].shape[0]
    share = attn_rows // page_devices
    sent = pack_blocks(
        part[0].reshape(*stage_sizes, share),
        part[1].reshape(*stage_sizes, share),
        part[2].reshape(*stage_sizes, share, HEAD_DIM),
        share,
    )
    for axis in STAGES:
        stage = merge_blocks(lax.all_to_all(sent, axis, 0, 0, tiled=False), share)
        sent = pack_blocks(*stage, share)
    top, total, acc = stage
    attended_mine = (acc / total[:, None]).astype(jnp.bfloat16)
    attended = gather_rows(attended_mine)
    flat_heads = attended.reshape(row_count, local_heads * PER_KV * HEAD_DIM)
    head_terms = jnp.dot(flat_heads, w_out, preferred_element_type=jnp.float32)
    mixed_out = jnp.sum(gather_all(head_terms, "kv"), axis=0) + widened
    return (mixed_out.astype(jnp.bfloat16).reshape(num_steps, num_seqs, -1), buffer)


def solution(mesh):
    row = mesh.devices[0]
    outer = len({device.coords[0] for device in row})
    split = Mesh(
        mesh.devices.reshape(mesh.devices.shape[0], outer, row.size // outer), ("kv",) + STAGES
    )
    pages = STAGES
    placed = (
        P(),
        P(),
        P(),
        P(),
        P("kv", pages),
        P(pages),
        P(pages, "kv"),
        P("kv", pages),
        P(None, None, None, "kv"),
        P(None, pages, None, "kv"),
    )
    return jax.shard_map(
        per_device,
        mesh=split,
        in_specs=placed,
        out_specs=(P(None, None, pages), P(None, None, None, "kv")),
        check_vma=False,
    )
```

```python
import jax
import jax.numpy as jnp
from jax import lax
from jax.sharding import Mesh, PartitionSpec as P

D = 7168
KV_HEADS = 8
HEAD_DIM = 128
GROUPS = 8
BEAMS = 8
PRIOR = 13
PAGE = 128
PER_KV = 7
HISTORY = 15
MAX_PAGES = 64


THETA = 5000000.0
EPSILON = 1e-05
NEGATIVE = -1e30


def rotate(values, positions):
    half_dim = HEAD_DIM // 2
    frequency = THETA ** (-(2.0 * jnp.arange(half_dim, dtype=jnp.float32)) / HEAD_DIM)
    angles = positions.astype(jnp.float32)[:, None] * frequency[None, :]
    cosine = jnp.cos(angles)[:, None, None, :]
    sine_part = jnp.sin(angles)[:, None, None, :]
    lower_part = values[..., :half_dim]
    upper_part = values[..., half_dim:]
    return jnp.concatenate(
        [
            lower_part * cosine - upper_part * sine_part,
            upper_part * cosine + lower_part * sine_part,
        ],
        axis=-1,
    )


def finish_rows(summed, norm_sums, row_ids, prompt_len, num_seqs, local_heads):
    inverse_rms = lax.rsqrt(norm_sums / D + EPSILON)
    projected = (summed * inverse_rms[:, None]).reshape(-1, local_heads, PER_KV + 2, HEAD_DIM)
    positions = jnp.take(prompt_len, row_ids % num_seqs // BEAMS) + PRIOR + row_ids // num_seqs
    turned = rotate(projected[:, :, : PER_KV + 1], positions)
    return jnp.concatenate([turned, projected[:, :, PER_KV + 1 :]], axis=2).astype(jnp.bfloat16)


def combine(earlier, later):
    peak = jnp.maximum(earlier[0], later[0])
    weight_one = jnp.exp(earlier[0] - peak)
    weight_two = jnp.exp(later[0] - peak)
    return (
        peak,
        earlier[1] * weight_one + later[1] * weight_two,
        earlier[2] * weight_one[:, None] + later[2] * weight_two[:, None],
    )


def gather_all(part, axis):
    count = lax.axis_size(axis)
    spread = jnp.broadcast_to(part[None], (count, *part.shape))
    return lax.all_to_all(spread, axis, 0, 0, tiled=False)


def gather_rows(part):
    inner = gather_all(part, "pz")
    inner = inner.reshape(-1, *part.shape[1:])
    outer = gather_all(inner, "px")
    return outer.reshape(-1, *part.shape[1:])


def reduce_rows(packed):
    for axis in ("px", "pz"):
        sources = lax.axis_size(axis)
        split = packed.reshape(sources, packed.shape[0] // sources, *packed.shape[1:])
        packed = jnp.sum(lax.all_to_all(split, axis, 0, 0, tiled=False), axis=0)
    return packed


def merge_blocks(received, share):
    peak = received[:, ..., share, :share]
    top = jnp.max(peak, axis=0)
    scale = jnp.exp(peak - top[None])
    total = jnp.sum(received[:, ..., share + 1, :share] * scale, axis=0)
    acc = jnp.sum(received[:, ..., :share, :] * scale[..., None], axis=0)
    return top, total, acc


def pack_blocks(top, total, acc, share):
    stats = jnp.zeros((*acc.shape[:-2], 2, HEAD_DIM), jnp.float32)
    stats = stats.at[..., 0, :share].set(top)
    stats = stats.at[..., 1, :share].set(total)
    return jnp.concatenate([acc, stats], axis=-2)


def per_device(
    tokens, prompt_len, page_table, parents, embedding, norm_gain, w_qkv, w_out, history, kv_pool
):
    num_steps, num_seqs = tokens.shape
    row_count = num_steps * num_seqs
    outer_count = lax.axis_size("px")
    inner_count = lax.axis_size("pz")
    page_devices = outer_count * inner_count
    page_index = lax.axis_index("px") * inner_count + lax.axis_index("pz")
    local_heads = KV_HEADS // lax.axis_size("kv")
    kv_width = local_heads * HEAD_DIM
    inv_root = 1.0 / jnp.sqrt(jnp.float32(HEAD_DIM))
    vocab_local = embedding.shape[0]
    local_ids = tokens.reshape(-1) - lax.axis_index("kv") * vocab_local
    inside = (local_ids >= 0) & (local_ids < vocab_local)
    picked = jnp.take(embedding, jnp.clip(local_ids, 0, vocab_local - 1), axis=0)
    found = jnp.where(inside[:, None], picked, jnp.zeros_like(picked))
    widened = jnp.sum(gather_all(found, "kv").astype(jnp.float32), axis=0)
    squares = jnp.sum(widened * widened, axis=1)
    normed = (widened * norm_gain.astype(jnp.float32)).astype(jnp.bfloat16)
    partial_value = jnp.dot(normed, w_qkv, preferred_element_type=jnp.float32)
    qkv_cols = partial_value.shape[1]
    packed = jnp.concatenate(
        [partial_value, squares[:, None], jnp.zeros((row_count, 127), jnp.float32)], axis=1
    )
    reduced = reduce_rows(packed)
    rows_per = row_count // page_devices
    my_rows = page_index * rows_per + jnp.arange(rows_per, dtype=jnp.int32)
    mine = finish_rows(
        reduced[:, :qkv_cols], reduced[:, qkv_cols], my_rows, prompt_len, num_seqs, local_heads
    )
    projected = gather_rows(mine.reshape(rows_per, qkv_cols)).reshape(
        row_count, local_heads, PER_KV + 2, HEAD_DIM
    )
    queries = projected[:, :, :PER_KV]
    fresh_kv = jnp.stack([projected[:, :, PER_KV], projected[:, :, PER_KV + 1]]).reshape(
        2, num_steps, num_seqs, kv_width
    )
    buffer = jnp.concatenate(
        [history, jnp.zeros((2, num_seqs, num_steps, kv_width), jnp.bfloat16)], axis=2
    )
    snapshots = []
    for step_index in range(num_steps):
        buffer = jnp.take(buffer, parents[step_index], axis=1)
        buffer = buffer.at[:, :, PRIOR + step_index].set(fresh_kv[:, step_index])
        snapshots.append(buffer)
    stacked = jnp.stack(snapshots)
    tail_keys = stacked[:, 0].reshape(num_steps, num_seqs, HISTORY, local_heads, HEAD_DIM)
    tail_vals = stacked[:, 1].reshape(num_steps, num_seqs, HISTORY, local_heads, HEAD_DIM)
    step_query = queries.reshape(num_steps, num_seqs, local_heads, PER_KV, HEAD_DIM)
    tail_len = PRIOR + 1 + jnp.arange(num_steps, dtype=jnp.int32)
    tail_valid = (jnp.arange(HISTORY, dtype=jnp.int32)[None, :] < tail_len[:, None])[
        :, None, None, None, :
    ]
    tail_scores = (
        jnp.einsum("tbkhd,tblkd->tbkhl", step_query, tail_keys, preferred_element_type=jnp.float32)
        * inv_root
    )
    tail_scores = jnp.where(tail_valid, tail_scores, NEGATIVE)
    tail_peak = jnp.max(tail_scores, axis=-1)
    tail_exp = jnp.where(tail_valid, jnp.exp(tail_scores - tail_peak[..., None]), 0.0)
    tail_total = jnp.sum(tail_exp, axis=-1)
    tail_acc = jnp.einsum(
        "tbkhl,tblkd->tbkhd",
        tail_exp.astype(jnp.bfloat16),
        tail_vals,
        preferred_element_type=jnp.float32,
    )
    tail_part = (tail_peak.reshape(-1), tail_total.reshape(-1), tail_acc.reshape(-1, HEAD_DIM))
    slot_rows = kv_pool.shape[1]
    slot_ids = page_index * slot_rows + jnp.arange(slot_rows, dtype=jnp.int32)
    matches = page_table[:, :, None] == slot_ids[None, None, :]
    slot_used = jnp.any(matches, axis=(0, 1))
    owner_group = jnp.sum(
        jnp.where(matches, jnp.arange(GROUPS, dtype=jnp.int32)[:, None, None], 0), axis=(0, 1)
    )
    page_number = jnp.sum(
        jnp.where(matches, jnp.arange(MAX_PAGES, dtype=jnp.int32)[None, :, None], 0), axis=(0, 1)
    )
    length = jnp.take(prompt_len, owner_group)
    live_tok = slot_used[:, None] & (
        page_number[:, None] * PAGE + jnp.arange(PAGE, dtype=jnp.int32)[None, :] < length[:, None]
    )
    live_full = live_tok[None, :, None, :]
    grouped = queries.reshape(num_steps, GROUPS, BEAMS, local_heads, PER_KV, HEAD_DIM)
    chosen = jnp.take(grouped, owner_group, axis=1)
    query_rows = num_steps * BEAMS * PER_KV
    chosen = jnp.transpose(chosen, (3, 1, 0, 2, 4, 5)).reshape(
        local_heads, slot_rows, query_rows, HEAD_DIM
    )
    page_keys = jnp.transpose(
        kv_pool[0].reshape(slot_rows, PAGE, local_heads, HEAD_DIM), (2, 0, 1, 3)
    )
    page_vals = jnp.transpose(
        kv_pool[1].reshape(slot_rows, PAGE, local_heads, HEAD_DIM), (2, 0, 1, 3)
    )
    scores = (
        jnp.einsum("ksqd,kspd->ksqp", chosen, page_keys, preferred_element_type=jnp.float32)
        * inv_root
    )
    scores = jnp.where(live_full, scores, NEGATIVE)
    slot_peak = jnp.max(scores, axis=-1)
    slot_exp = jnp.where(live_full, jnp.exp(scores - slot_peak[..., None]), 0.0)
    slot_total = jnp.sum(slot_exp, axis=-1)
    slot_acc = jnp.einsum(
        "ksqp,kspd->ksqd",
        slot_exp.astype(jnp.bfloat16),
        page_vals,
        preferred_element_type=jnp.float32,
    )
    member = (owner_group[:, None] == jnp.arange(GROUPS, dtype=jnp.int32)[None, :]) & slot_used[
        :, None
    ]
    spread = jnp.where(member[None, :, :, None], slot_peak[:, :, None, :], NEGATIVE)
    group_peak = jnp.max(spread, axis=1)
    slot_base = jnp.take(group_peak, owner_group, axis=1)
    weight = jnp.where(slot_used[None, :, None], jnp.exp(slot_peak - slot_base), 0.0)
    member_f = member.astype(jnp.float32)
    group_total = jnp.einsum(
        "sg,ksq->kgq", member_f, slot_total * weight, precision=lax.Precision.HIGHEST
    )
    group_acc = jnp.einsum(
        "sg,ksqd->kgqd", member_f, slot_acc * weight[..., None], precision=lax.Precision.HIGHEST
    )
    order_small = (2, 1, 3, 0, 4)
    peak_rows = jnp.transpose(
        group_peak.reshape(local_heads, GROUPS, num_steps, BEAMS, PER_KV), order_small
    )
    total_rows = jnp.transpose(
        group_total.reshape(local_heads, GROUPS, num_steps, BEAMS, PER_KV), order_small
    )
    acc_rows = jnp.transpose(
        group_acc.reshape(local_heads, GROUPS, num_steps, BEAMS, PER_KV, HEAD_DIM),
        (2, 1, 3, 0, 4, 5),
    )
    local_part = (peak_rows.reshape(-1), total_rows.reshape(-1), acc_rows.reshape(-1, HEAD_DIM))
    with_tail = combine(local_part, tail_part)
    first = page_index == 0
    part = jax.tree.map(lambda a, b: jnp.where(first, a, b), with_tail, local_part)
    attn_rows = part[0].shape[0]
    share = attn_rows // page_devices
    sent = pack_blocks(
        part[0].reshape(outer_count, inner_count, share),
        part[1].reshape(outer_count, inner_count, share),
        part[2].reshape(outer_count, inner_count, share, HEAD_DIM),
        share,
    )
    stage = merge_blocks(lax.all_to_all(sent, "px", 0, 0, tiled=False), share)
    sent = pack_blocks(*stage, share)
    top, total, acc = merge_blocks(lax.all_to_all(sent, "pz", 0, 0, tiled=False), share)
    attended_mine = (acc / total[:, None]).astype(jnp.bfloat16)
    attended = gather_rows(attended_mine)
    flat_heads = attended.reshape(row_count, local_heads * PER_KV * HEAD_DIM)
    head_terms = jnp.dot(flat_heads, w_out, preferred_element_type=jnp.float32)
    shared = gather_all(head_terms.astype(jnp.bfloat16), "kv").astype(jnp.float32)
    mixed_out = jnp.sum(shared, axis=0) + widened
    return (mixed_out.astype(jnp.bfloat16).reshape(num_steps, num_seqs, -1), buffer)


def solution(mesh):
    row = mesh.devices[0]
    outer = len({device.coords[0] for device in row})
    split = Mesh(
        mesh.devices.reshape(mesh.devices.shape[0], outer, row.size // outer), ("kv", "px", "pz")
    )
    pages = ("px", "pz")
    placed = (
        P(),
        P(),
        P(),
        P(),
        P("kv", pages),
        P(pages),
        P(pages, "kv"),
        P("kv", pages),
        P(None, None, None, "kv"),
        P(None, pages, None, "kv"),
    )
    return jax.shard_map(
        per_device,
        mesh=split,
        in_specs=placed,
        out_specs=(P(None, None, pages), P(None, None, None, "kv")),
        check_vma=False,
    )
```

```python
import jax
import jax.numpy as jnp
from jax import lax
from jax.sharding import Mesh, PartitionSpec as P

D = 7168
KV_HEADS = 8
HEAD_DIM = 128
GROUPS = 8
BEAMS = 8
PRIOR = 13
PAGE = 128
PER_KV = 7
HISTORY = 15
MAX_PAGES = 64


THETA = 5000000.0
EPSILON = 1e-05
NEGATIVE = -1e30


def rotate(values, positions):
    half_dim = HEAD_DIM // 2
    frequency = THETA ** (-(2.0 * jnp.arange(half_dim, dtype=jnp.float32)) / HEAD_DIM)
    angles = positions.astype(jnp.float32)[:, None] * frequency[None, :]
    cosine = jnp.cos(angles)[:, None, None, :]
    sine_part = jnp.sin(angles)[:, None, None, :]
    lower_part = values[..., :half_dim]
    upper_part = values[..., half_dim:]
    return jnp.concatenate(
        [
            lower_part * cosine - upper_part * sine_part,
            upper_part * cosine + lower_part * sine_part,
        ],
        axis=-1,
    )


def finish_rows(summed, norm_sums, row_ids, prompt_len, num_seqs, local_heads):
    inverse_rms = lax.rsqrt(norm_sums / D + EPSILON)
    projected = (summed * inverse_rms[:, None]).reshape(-1, local_heads, PER_KV + 2, HEAD_DIM)
    positions = jnp.take(prompt_len, row_ids % num_seqs // BEAMS) + PRIOR + row_ids // num_seqs
    turned = rotate(projected[:, :, : PER_KV + 1], positions)
    return jnp.concatenate([turned, projected[:, :, PER_KV + 1 :]], axis=2).astype(jnp.bfloat16)


def combine(earlier, later):
    peak = jnp.maximum(earlier[0], later[0])
    weight_one = jnp.exp(earlier[0] - peak)
    weight_two = jnp.exp(later[0] - peak)
    return (
        peak,
        earlier[1] * weight_one + later[1] * weight_two,
        earlier[2] * weight_one[:, None] + later[2] * weight_two[:, None],
    )


def gather_all(part, axis):
    count = lax.axis_size(axis)
    spread = jnp.broadcast_to(part[None], (count, *part.shape))
    return lax.all_to_all(spread, axis, 0, 0, tiled=False)


def gather_rows(part):
    inner = gather_all(part, "pz")
    inner = inner.reshape(-1, *part.shape[1:])
    outer = gather_all(inner, "px")
    return outer.reshape(-1, *part.shape[1:])


def reduce_rows(packed):
    for axis in ("px", "pz"):
        sources = lax.axis_size(axis)
        split = packed.reshape(sources, packed.shape[0] // sources, *packed.shape[1:])
        packed = jnp.sum(lax.all_to_all(split, axis, 0, 0, tiled=False), axis=0)
    return packed


def merge_blocks(received, share):
    peak = received[:, ..., share, :share]
    top = jnp.max(peak, axis=0)
    scale = jnp.exp(peak - top[None])
    total = jnp.sum(received[:, ..., share + 1, :share] * scale, axis=0)
    acc = jnp.sum(received[:, ..., :share, :] * scale[..., None], axis=0)
    return top, total, acc


def pack_blocks(top, total, acc, share):
    widths = [(0, 0)] * (top.ndim - 1) + [(0, HEAD_DIM - share)]
    stats = jnp.stack([jnp.pad(top, widths), jnp.pad(total, widths)], axis=-2)
    return jnp.concatenate([acc, stats], axis=-2)


def per_device(
    tokens, prompt_len, page_table, parents, embedding, norm_gain, w_qkv, w_out, history, kv_pool
):
    num_steps, num_seqs = tokens.shape
    row_count = num_steps * num_seqs
    outer_count = lax.axis_size("px")
    inner_count = lax.axis_size("pz")
    page_devices = outer_count * inner_count
    page_index = lax.axis_index("px") * inner_count + lax.axis_index("pz")
    local_heads = KV_HEADS // lax.axis_size("kv")
    kv_width = local_heads * HEAD_DIM
    inv_root = 1.0 / jnp.sqrt(jnp.float32(HEAD_DIM))
    vocab_local = embedding.shape[0]
    local_ids = tokens.reshape(-1) - lax.axis_index("kv") * vocab_local
    pick = local_ids[:, None] == jnp.arange(vocab_local, dtype=jnp.int32)[None, :]
    found = jnp.dot(
        pick.astype(jnp.bfloat16), embedding, preferred_element_type=jnp.float32
    ).astype(jnp.bfloat16)
    widened = jnp.sum(gather_all(found, "kv").astype(jnp.float32), axis=0)
    squares = jnp.sum(widened * widened, axis=1)
    normed = (widened * norm_gain.astype(jnp.float32)).astype(jnp.bfloat16)
    partial_value = jnp.dot(normed, w_qkv, preferred_element_type=jnp.float32)
    qkv_cols = partial_value.shape[1]
    packed = jnp.concatenate(
        [partial_value, squares[:, None], jnp.zeros((row_count, 127), jnp.float32)], axis=1
    )
    reduced = reduce_rows(packed)
    rows_per = row_count // page_devices
    my_rows = page_index * rows_per + jnp.arange(rows_per, dtype=jnp.int32)
    mine = finish_rows(
        reduced[:, :qkv_cols], reduced[:, qkv_cols], my_rows, prompt_len, num_seqs, local_heads
    )
    projected = gather_rows(mine.reshape(rows_per, qkv_cols)).reshape(
        row_count, local_heads, PER_KV + 2, HEAD_DIM
    )
    queries = projected[:, :, :PER_KV]
    fresh_kv = jnp.stack([projected[:, :, PER_KV], projected[:, :, PER_KV + 1]]).reshape(
        2, num_steps, num_seqs, kv_width
    )
    buffer = jnp.concatenate(
        [history, jnp.zeros((2, num_seqs, num_steps, kv_width), jnp.bfloat16)], axis=2
    )
    snapshots = []
    for step_index in range(num_steps):
        choose = parents[step_index][:, None] == jnp.arange(num_seqs, dtype=jnp.int32)[None, :]
        buffer = jnp.einsum(
            "nb,kbld->knld",
            choose.astype(jnp.bfloat16),
            buffer,
            preferred_element_type=jnp.float32,
        ).astype(jnp.bfloat16)
        buffer = lax.dynamic_update_slice(
            buffer, fresh_kv[:, step_index][:, :, None, :], (0, 0, PRIOR + step_index, 0)
        )
        snapshots.append(buffer)
    stacked = jnp.stack(snapshots)
    tail_keys = stacked[:, 0].reshape(num_steps, num_seqs, HISTORY, local_heads, HEAD_DIM)
    tail_vals = stacked[:, 1].reshape(num_steps, num_seqs, HISTORY, local_heads, HEAD_DIM)
    step_query = queries.reshape(num_steps, num_seqs, local_heads, PER_KV, HEAD_DIM)
    tail_len = PRIOR + 1 + jnp.arange(num_steps, dtype=jnp.int32)
    tail_valid = (jnp.arange(HISTORY, dtype=jnp.int32)[None, :] < tail_len[:, None])[
        :, None, None, None, :
    ]
    tail_scores = (
        jnp.einsum("tbkhd,tblkd->tbkhl", step_query, tail_keys, preferred_element_type=jnp.float32)
        * inv_root
    )
    tail_scores = jnp.where(tail_valid, tail_scores, NEGATIVE)
    tail_peak = jnp.max(tail_scores, axis=-1)
    tail_exp = jnp.where(tail_valid, jnp.exp(tail_scores - tail_peak[..., None]), 0.0)
    tail_total = jnp.sum(tail_exp, axis=-1)
    tail_acc = jnp.einsum(
        "tbkhl,tblkd->tbkhd",
        tail_exp.astype(jnp.bfloat16),
        tail_vals,
        preferred_element_type=jnp.float32,
    )
    tail_part = (tail_peak.reshape(-1), tail_total.reshape(-1), tail_acc.reshape(-1, HEAD_DIM))
    slot_rows = kv_pool.shape[1]
    slot_ids = page_index * slot_rows + jnp.arange(slot_rows, dtype=jnp.int32)
    matches = page_table[:, :, None] == slot_ids[None, None, :]
    slot_used = jnp.any(matches, axis=(0, 1))
    owner_group = jnp.sum(
        jnp.where(matches, jnp.arange(GROUPS, dtype=jnp.int32)[:, None, None], 0), axis=(0, 1)
    )
    page_number = jnp.sum(
        jnp.where(matches, jnp.arange(MAX_PAGES, dtype=jnp.int32)[None, :, None], 0), axis=(0, 1)
    )
    length = jnp.take(prompt_len, owner_group)
    live_tok = slot_used[:, None] & (
        page_number[:, None] * PAGE + jnp.arange(PAGE, dtype=jnp.int32)[None, :] < length[:, None]
    )
    live_full = live_tok[None, :, None, :]
    grouped = queries.reshape(num_steps, GROUPS, BEAMS, local_heads, PER_KV, HEAD_DIM)
    chosen = jnp.take(grouped, owner_group, axis=1)
    query_rows = num_steps * BEAMS * PER_KV
    chosen = jnp.transpose(chosen, (3, 1, 0, 2, 4, 5)).reshape(
        local_heads, slot_rows, query_rows, HEAD_DIM
    )
    page_keys = jnp.transpose(
        kv_pool[0].reshape(slot_rows, PAGE, local_heads, HEAD_DIM), (2, 0, 1, 3)
    )
    page_vals = jnp.transpose(
        kv_pool[1].reshape(slot_rows, PAGE, local_heads, HEAD_DIM), (2, 0, 1, 3)
    )
    scores = (
        jnp.einsum("ksqd,kspd->ksqp", chosen, page_keys, preferred_element_type=jnp.float32)
        * inv_root
    )
    scores = jnp.where(live_full, scores, NEGATIVE)
    slot_peak = jnp.max(scores, axis=-1)
    slot_exp = jnp.where(live_full, jnp.exp(scores - slot_peak[..., None]), 0.0)
    slot_total = jnp.sum(slot_exp, axis=-1)
    slot_acc = jnp.einsum(
        "ksqp,kspd->ksqd",
        slot_exp.astype(jnp.bfloat16),
        page_vals,
        preferred_element_type=jnp.float32,
    )
    member = (owner_group[:, None] == jnp.arange(GROUPS, dtype=jnp.int32)[None, :]) & slot_used[
        :, None
    ]
    spread = jnp.where(member[None, :, :, None], slot_peak[:, :, None, :], NEGATIVE)
    group_peak = jnp.max(spread, axis=1)
    slot_base = jnp.take(group_peak, owner_group, axis=1)
    weight = jnp.where(slot_used[None, :, None], jnp.exp(slot_peak - slot_base), 0.0)
    member_f = member.astype(jnp.float32)
    group_total = jnp.einsum(
        "sg,ksq->kgq", member_f, slot_total * weight, precision=lax.Precision.HIGHEST
    )
    group_acc = jnp.einsum(
        "sg,ksqd->kgqd", member_f, slot_acc * weight[..., None], precision=lax.Precision.HIGHEST
    )
    order_small = (2, 1, 3, 0, 4)
    peak_rows = jnp.transpose(
        group_peak.reshape(local_heads, GROUPS, num_steps, BEAMS, PER_KV), order_small
    )
    total_rows = jnp.transpose(
        group_total.reshape(local_heads, GROUPS, num_steps, BEAMS, PER_KV), order_small
    )
    acc_rows = jnp.transpose(
        group_acc.reshape(local_heads, GROUPS, num_steps, BEAMS, PER_KV, HEAD_DIM),
        (2, 1, 3, 0, 4, 5),
    )
    local_part = (peak_rows.reshape(-1), total_rows.reshape(-1), acc_rows.reshape(-1, HEAD_DIM))
    with_tail = combine(local_part, tail_part)
    first = page_index == 0
    part = jax.tree.map(lambda a, b: jnp.where(first, a, b), with_tail, local_part)
    attn_rows = part[0].shape[0]
    share = attn_rows // page_devices
    sent = pack_blocks(
        part[0].reshape(outer_count, inner_count, share),
        part[1].reshape(outer_count, inner_count, share),
        part[2].reshape(outer_count, inner_count, share, HEAD_DIM),
        share,
    )
    stage = merge_blocks(lax.all_to_all(sent, "px", 0, 0, tiled=False), share)
    sent = pack_blocks(*stage, share)
    top, total, acc = merge_blocks(lax.all_to_all(sent, "pz", 0, 0, tiled=False), share)
    attended_mine = (acc / total[:, None]).astype(jnp.bfloat16)
    attended = gather_rows(attended_mine)
    flat_heads = attended.reshape(row_count, local_heads * PER_KV * HEAD_DIM)
    head_terms = jnp.dot(flat_heads, w_out, preferred_element_type=jnp.float32)
    shared = gather_all(head_terms.astype(jnp.bfloat16), "kv").astype(jnp.float32)
    mixed_out = jnp.sum(shared, axis=0) + widened
    return (mixed_out.astype(jnp.bfloat16).reshape(num_steps, num_seqs, -1), buffer)


def solution(mesh):
    row = mesh.devices[0]
    outer = len({device.coords[0] for device in row})
    split = Mesh(
        mesh.devices.reshape(mesh.devices.shape[0], outer, row.size // outer), ("kv", "px", "pz")
    )
    pages = ("px", "pz")
    placed = (
        P(),
        P(),
        P(),
        P(),
        P("kv", pages),
        P(pages),
        P(pages, "kv"),
        P("kv", pages),
        P(None, None, None, "kv"),
        P(None, pages, None, "kv"),
    )
    return jax.shard_map(
        per_device,
        mesh=split,
        in_specs=placed,
        out_specs=(P(None, None, pages), P(None, None, None, "kv")),
        check_vma=False,
    )
```

```python
import jax
import jax.numpy as jnp
from jax import lax
from jax.sharding import Mesh, PartitionSpec as P

D = 7168
KV_HEADS = 8
HEAD_DIM = 128
GROUPS = 8
BEAMS = 8
PRIOR = 13
PAGE = 128
PER_KV = 7
HISTORY = 15
MAX_PAGES = 64


THETA = 5000000.0
EPSILON = 1e-05
NEGATIVE = -1e30


def rotate(values, positions):
    half_dim = HEAD_DIM // 2
    frequency = THETA ** (-(2.0 * jnp.arange(half_dim, dtype=jnp.float32)) / HEAD_DIM)
    angles = positions.astype(jnp.float32)[:, None] * frequency[None, :]
    cosine = jnp.cos(angles)[:, None, None, :]
    sine_part = jnp.sin(angles)[:, None, None, :]
    lower_part = values[..., :half_dim]
    upper_part = values[..., half_dim:]
    return jnp.concatenate(
        [
            lower_part * cosine - upper_part * sine_part,
            upper_part * cosine + lower_part * sine_part,
        ],
        axis=-1,
    )


def finish_rows(summed, norm_sums, row_ids, prompt_len, num_seqs, local_heads):
    inverse_rms = lax.rsqrt(norm_sums / D + EPSILON)
    projected = (summed * inverse_rms[:, None]).reshape(-1, local_heads, PER_KV + 2, HEAD_DIM)
    positions = jnp.take(prompt_len, row_ids % num_seqs // BEAMS) + PRIOR + row_ids // num_seqs
    turned = rotate(projected[:, :, : PER_KV + 1], positions)
    return jnp.concatenate([turned, projected[:, :, PER_KV + 1 :]], axis=2).astype(jnp.bfloat16)


def combine(earlier, later):
    peak = jnp.maximum(earlier[0], later[0])
    weight_one = jnp.exp(earlier[0] - peak)
    weight_two = jnp.exp(later[0] - peak)
    return (
        peak,
        earlier[1] * weight_one + later[1] * weight_two,
        earlier[2] * weight_one[:, None] + later[2] * weight_two[:, None],
    )


def gather_all(part, axis):
    count = lax.axis_size(axis)
    spread = jnp.broadcast_to(part[None], (count, *part.shape))
    return lax.all_to_all(spread, axis, 0, 0, tiled=False)


def gather_rows(part):
    inner = gather_all(part, "pz")
    inner = inner.reshape(-1, *part.shape[1:])
    outer = gather_all(inner, "px")
    return outer.reshape(-1, *part.shape[1:])


def reduce_rows(packed):
    for axis in ("px", "pz"):
        sources = lax.axis_size(axis)
        split = packed.reshape(sources, packed.shape[0] // sources, *packed.shape[1:])
        packed = jnp.sum(lax.all_to_all(split, axis, 0, 0, tiled=False), axis=0)
    return packed


def merge_blocks(received, share):
    peak = received[:, ..., share, :share]
    top = jnp.max(peak, axis=0)
    scale = jnp.exp(peak - top[None])
    total = jnp.sum(received[:, ..., share + 1, :share] * scale, axis=0)
    acc = jnp.sum(received[:, ..., :share, :] * scale[..., None], axis=0)
    return top, total, acc


def pack_blocks(top, total, acc, share):
    widths = [(0, 0)] * (top.ndim - 1) + [(0, HEAD_DIM - share)]
    stats = jnp.stack([jnp.pad(top, widths), jnp.pad(total, widths)], axis=-2)
    return jnp.concatenate([acc, stats], axis=-2)


def per_device(
    tokens, prompt_len, page_table, parents, embedding, norm_gain, w_qkv, w_out, history, kv_pool
):
    num_steps, num_seqs = tokens.shape
    row_count = num_steps * num_seqs
    outer_count = lax.axis_size("px")
    inner_count = lax.axis_size("pz")
    page_devices = outer_count * inner_count
    page_index = lax.axis_index("px") * inner_count + lax.axis_index("pz")
    local_heads = KV_HEADS // lax.axis_size("kv")
    kv_width = local_heads * HEAD_DIM
    inv_root = 1.0 / jnp.sqrt(jnp.float32(HEAD_DIM))
    vocab_local = embedding.shape[0]
    local_ids = tokens.reshape(-1) - lax.axis_index("kv") * vocab_local
    pick = local_ids[:, None] == jnp.arange(vocab_local, dtype=jnp.int32)[None, :]
    found = jnp.dot(
        pick.astype(jnp.bfloat16), embedding, preferred_element_type=jnp.float32
    ).astype(jnp.bfloat16)
    widened = jnp.sum(gather_all(found, "kv").astype(jnp.float32), axis=0)
    squares = jnp.sum(widened * widened, axis=1)
    normed = (widened * norm_gain.astype(jnp.float32)).astype(jnp.bfloat16)
    partial_value = jnp.dot(normed, w_qkv, preferred_element_type=jnp.float32)
    qkv_cols = partial_value.shape[1]
    packed = jnp.concatenate(
        [partial_value, squares[:, None], jnp.zeros((row_count, 127), jnp.float32)], axis=1
    )
    reduced = reduce_rows(packed)
    rows_per = row_count // page_devices
    my_rows = page_index * rows_per + jnp.arange(rows_per, dtype=jnp.int32)
    mine = finish_rows(
        reduced[:, :qkv_cols], reduced[:, qkv_cols], my_rows, prompt_len, num_seqs, local_heads
    )
    projected = gather_rows(mine.reshape(rows_per, qkv_cols)).reshape(
        row_count, local_heads, PER_KV + 2, HEAD_DIM
    )
    queries = projected[:, :, :PER_KV]
    fresh_kv = jnp.stack([projected[:, :, PER_KV], projected[:, :, PER_KV + 1]]).reshape(
        2, num_steps, num_seqs, kv_width
    )
    buffer = jnp.concatenate(
        [history, jnp.zeros((2, num_seqs, num_steps, kv_width), jnp.bfloat16)], axis=2
    )
    snapshots = []
    for step_index in range(num_steps):
        choose = parents[step_index][:, None] == jnp.arange(num_seqs, dtype=jnp.int32)[None, :]
        buffer = jnp.einsum(
            "nb,kbld->knld",
            choose.astype(jnp.bfloat16),
            buffer,
            preferred_element_type=jnp.float32,
        ).astype(jnp.bfloat16)
        buffer = lax.dynamic_update_slice(
            buffer, fresh_kv[:, step_index][:, :, None, :], (0, 0, PRIOR + step_index, 0)
        )
        snapshots.append(buffer)
    stacked = jnp.stack(snapshots)
    tail_keys = stacked[:, 0].reshape(num_steps, num_seqs, HISTORY, local_heads, HEAD_DIM)
    tail_vals = stacked[:, 1].reshape(num_steps, num_seqs, HISTORY, local_heads, HEAD_DIM)
    step_query = queries.reshape(num_steps, num_seqs, local_heads, PER_KV, HEAD_DIM)
    tail_len = PRIOR + 1 + jnp.arange(num_steps, dtype=jnp.int32)
    tail_valid = (jnp.arange(HISTORY, dtype=jnp.int32)[None, :] < tail_len[:, None])[
        :, None, None, None, :
    ]
    tail_scores = (
        jnp.einsum("tbkhd,tblkd->tbkhl", step_query, tail_keys, preferred_element_type=jnp.float32)
        * inv_root
    )
    tail_scores = jnp.where(tail_valid, tail_scores, NEGATIVE)
    tail_peak = jnp.max(tail_scores, axis=-1)
    tail_exp = jnp.where(tail_valid, jnp.exp(tail_scores - tail_peak[..., None]), 0.0)
    tail_total = jnp.sum(tail_exp, axis=-1)
    tail_acc = jnp.einsum(
        "tbkhl,tblkd->tbkhd",
        tail_exp.astype(jnp.bfloat16),
        tail_vals,
        preferred_element_type=jnp.float32,
    )
    tail_part = (tail_peak.reshape(-1), tail_total.reshape(-1), tail_acc.reshape(-1, HEAD_DIM))
    slot_rows = kv_pool.shape[1]
    slot_ids = page_index * slot_rows + jnp.arange(slot_rows, dtype=jnp.int32)
    matches = page_table[:, :, None] == slot_ids[None, None, :]
    slot_used = jnp.any(matches, axis=(0, 1))
    owner_group = jnp.sum(
        jnp.where(matches, jnp.arange(GROUPS, dtype=jnp.int32)[:, None, None], 0), axis=(0, 1)
    )
    page_number = jnp.sum(
        jnp.where(matches, jnp.arange(MAX_PAGES, dtype=jnp.int32)[None, :, None], 0), axis=(0, 1)
    )
    length = jnp.take(prompt_len, owner_group)
    live_tok = slot_used[:, None] & (
        page_number[:, None] * PAGE + jnp.arange(PAGE, dtype=jnp.int32)[None, :] < length[:, None]
    )
    live_full = live_tok[None, :, None, :]
    grouped = queries.reshape(num_steps, GROUPS, BEAMS, local_heads, PER_KV, HEAD_DIM)
    owner = owner_group[:, None] == jnp.arange(GROUPS, dtype=jnp.int32)[None, :]
    chosen = jnp.einsum(
        "sg,tgbkhd->tsbkhd",
        owner.astype(jnp.bfloat16),
        grouped,
        preferred_element_type=jnp.float32,
    ).astype(jnp.bfloat16)
    query_rows = num_steps * BEAMS * PER_KV
    chosen = jnp.transpose(chosen, (3, 1, 0, 2, 4, 5)).reshape(
        local_heads, slot_rows, query_rows, HEAD_DIM
    )
    page_keys = jnp.transpose(
        kv_pool[0].reshape(slot_rows, PAGE, local_heads, HEAD_DIM), (2, 0, 1, 3)
    )
    page_vals = jnp.transpose(
        kv_pool[1].reshape(slot_rows, PAGE, local_heads, HEAD_DIM), (2, 0, 1, 3)
    )
    scores = (
        jnp.einsum("ksqd,kspd->ksqp", chosen, page_keys, preferred_element_type=jnp.float32)
        * inv_root
    )
    scores = jnp.where(live_full, scores, NEGATIVE)
    slot_peak = jnp.max(scores, axis=-1)
    slot_exp = jnp.where(live_full, jnp.exp(scores - slot_peak[..., None]), 0.0)
    slot_total = jnp.sum(slot_exp, axis=-1)
    slot_acc = jnp.einsum(
        "ksqp,kspd->ksqd",
        slot_exp.astype(jnp.bfloat16),
        page_vals,
        preferred_element_type=jnp.float32,
    )
    member = (owner_group[:, None] == jnp.arange(GROUPS, dtype=jnp.int32)[None, :]) & slot_used[
        :, None
    ]
    spread = jnp.where(member[None, :, :, None], slot_peak[:, :, None, :], NEGATIVE)
    group_peak = jnp.max(spread, axis=1)
    slot_base = jnp.max(
        jnp.where(owner[None, :, :, None], group_peak[:, None, :, :], -jnp.inf), axis=2
    )
    weight = jnp.where(slot_used[None, :, None], jnp.exp(slot_peak - slot_base), 0.0)
    member_f = member.astype(jnp.float32)
    group_total = jnp.einsum(
        "sg,ksq->kgq", member_f, slot_total * weight, precision=lax.Precision.HIGHEST
    )
    group_acc = jnp.einsum(
        "sg,ksqd->kgqd", member_f, slot_acc * weight[..., None], precision=lax.Precision.HIGHEST
    )
    order_small = (2, 1, 3, 0, 4)
    peak_rows = jnp.transpose(
        group_peak.reshape(local_heads, GROUPS, num_steps, BEAMS, PER_KV), order_small
    )
    total_rows = jnp.transpose(
        group_total.reshape(local_heads, GROUPS, num_steps, BEAMS, PER_KV), order_small
    )
    acc_rows = jnp.transpose(
        group_acc.reshape(local_heads, GROUPS, num_steps, BEAMS, PER_KV, HEAD_DIM),
        (2, 1, 3, 0, 4, 5),
    )
    local_part = (peak_rows.reshape(-1), total_rows.reshape(-1), acc_rows.reshape(-1, HEAD_DIM))
    with_tail = combine(local_part, tail_part)
    first = page_index == 0
    part = jax.tree.map(lambda a, b: jnp.where(first, a, b), with_tail, local_part)
    attn_rows = part[0].shape[0]
    share = attn_rows // page_devices
    sent = pack_blocks(
        part[0].reshape(outer_count, inner_count, share),
        part[1].reshape(outer_count, inner_count, share),
        part[2].reshape(outer_count, inner_count, share, HEAD_DIM),
        share,
    )
    stage = merge_blocks(lax.all_to_all(sent, "px", 0, 0, tiled=False), share)
    sent = pack_blocks(*stage, share)
    top, total, acc = merge_blocks(lax.all_to_all(sent, "pz", 0, 0, tiled=False), share)
    inner_spread = (inner_count, *acc.shape)
    attended_mine = (
        jnp.broadcast_to(acc[None], inner_spread) / jnp.broadcast_to(total[None, :, None], inner_spread)
    ).astype(jnp.bfloat16)
    attended = lax.all_to_all(attended_mine, "pz", 0, 0, tiled=False).reshape(-1, HEAD_DIM)
    attended = gather_all(attended, "px").reshape(-1, HEAD_DIM)
    flat_heads = attended.reshape(row_count, local_heads * PER_KV * HEAD_DIM)
    head_terms = jnp.dot(flat_heads, w_out, preferred_element_type=jnp.float32)
    shared = gather_all(head_terms.astype(jnp.bfloat16), "kv").astype(jnp.float32)
    mixed_out = jnp.sum(shared, axis=0) + widened
    return (mixed_out.astype(jnp.bfloat16).reshape(num_steps, num_seqs, -1), buffer)


def solution(mesh):
    row = mesh.devices[0]
    outer = len({device.coords[0] for device in row})
    split = Mesh(
        mesh.devices.reshape(mesh.devices.shape[0], outer, row.size // outer), ("kv", "px", "pz")
    )
    pages = ("px", "pz")
    placed = (
        P(),
        P(),
        P(),
        P(),
        P("kv", pages),
        P(pages),
        P(pages, "kv"),
        P("kv", pages),
        P(None, None, None, "kv"),
        P(None, pages, None, "kv"),
    )
    return jax.shard_map(
        per_device,
        mesh=split,
        in_specs=placed,
        out_specs=(P(None, None, pages), P(None, None, None, "kv")),
        check_vma=False,
    )
```

```python
import jax
import jax.numpy as jnp
from jax import lax
from jax.sharding import Mesh, PartitionSpec as P

D = 7168
KV_HEADS = 8
HEAD_DIM = 128
GROUPS = 8
BEAMS = 8
PRIOR = 13
PAGE = 128
PER_KV = 7
HISTORY = 15
MAX_PAGES = 64


THETA = 5000000.0
EPSILON = 1e-05
NEGATIVE = -1e30


def rotate(values, positions):
    half_dim = HEAD_DIM // 2
    frequency = THETA ** (-(2.0 * jnp.arange(half_dim, dtype=jnp.float32)) / HEAD_DIM)
    angles = positions.astype(jnp.float32)[:, None] * frequency[None, :]
    cosine = jnp.cos(angles)[:, None, None, :]
    sine_part = jnp.sin(angles)[:, None, None, :]
    lower_part = values[..., :half_dim]
    upper_part = values[..., half_dim:]
    return jnp.concatenate(
        [
            lower_part * cosine - upper_part * sine_part,
            upper_part * cosine + lower_part * sine_part,
        ],
        axis=-1,
    )


def finish_rows(summed, norm_sums, row_ids, prompt_len, num_seqs, local_heads):
    inverse_rms = lax.rsqrt(norm_sums / D + EPSILON)
    projected = (summed * inverse_rms[:, None]).reshape(-1, local_heads, PER_KV + 2, HEAD_DIM)
    positions = jnp.take(prompt_len, row_ids % num_seqs // BEAMS) + PRIOR + row_ids // num_seqs
    turned = rotate(projected[:, :, : PER_KV + 1], positions)
    return jnp.concatenate([turned, projected[:, :, PER_KV + 1 :]], axis=2).astype(jnp.bfloat16)


def combine(earlier, later):
    peak = jnp.maximum(earlier[0], later[0])
    weight_one = jnp.exp(earlier[0] - peak)
    weight_two = jnp.exp(later[0] - peak)
    return (
        peak,
        earlier[1] * weight_one + later[1] * weight_two,
        earlier[2] * weight_one[:, None] + later[2] * weight_two[:, None],
    )


def gather_all(part, axis):
    count = lax.axis_size(axis)
    spread = jnp.broadcast_to(part[None], (count, *part.shape))
    return lax.all_to_all(spread, axis, 0, 0, tiled=False)


def gather_rows(part):
    lanes = part.reshape(-1, HEAD_DIM)
    inner = gather_all(lanes, "pz")
    inner = inner.reshape(-1, *part.shape[1:])
    outer = gather_all(inner, "px")
    return outer.reshape(-1, *part.shape[1:])


def reduce_rows(packed):
    for axis in ("px", "pz"):
        sources = lax.axis_size(axis)
        block = (packed.shape[0] // sources, *packed.shape[1:])
        split = packed.reshape(sources, -1, HEAD_DIM)
        packed = jnp.sum(lax.all_to_all(split, axis, 0, 0, tiled=False), axis=0).reshape(block)
    return packed


def merge_blocks(received, share):
    peak = received[:, ..., share, :share]
    top = jnp.max(peak, axis=0)
    scale = jnp.exp(peak - top[None])
    total = jnp.sum(received[:, ..., share + 1, :share] * scale, axis=0)
    acc = jnp.sum(received[:, ..., :share, :] * scale[..., None], axis=0)
    return top, total, acc


def pack_blocks(top, total, acc, share):
    widths = [(0, 0)] * (top.ndim - 1) + [(0, HEAD_DIM - share)]
    stats = jnp.stack([jnp.pad(top, widths), jnp.pad(total, widths)], axis=-2)
    return jnp.concatenate([acc, stats], axis=-2)


def per_device(
    tokens, prompt_len, page_table, parents, embedding, norm_gain, w_qkv, w_out, history, kv_pool
):
    num_steps, num_seqs = tokens.shape
    row_count = num_steps * num_seqs
    outer_count = lax.axis_size("px")
    inner_count = lax.axis_size("pz")
    page_devices = outer_count * inner_count
    page_index = lax.axis_index("px") * inner_count + lax.axis_index("pz")
    local_heads = KV_HEADS // lax.axis_size("kv")
    kv_width = local_heads * HEAD_DIM
    inv_root = 1.0 / jnp.sqrt(jnp.float32(HEAD_DIM))
    vocab_local = embedding.shape[0]
    local_ids = tokens.reshape(-1) - lax.axis_index("kv") * vocab_local
    pick = local_ids[:, None] == jnp.arange(vocab_local, dtype=jnp.int32)[None, :]
    found = jnp.dot(
        pick.astype(jnp.bfloat16), embedding, preferred_element_type=jnp.float32
    ).astype(jnp.bfloat16)
    widened = jnp.sum(gather_all(found, "kv").astype(jnp.float32), axis=0)
    squares = jnp.sum(widened * widened, axis=1)
    normed = (widened * norm_gain.astype(jnp.float32)).astype(jnp.bfloat16)
    partial_value = jnp.dot(normed, w_qkv, preferred_element_type=jnp.float32)
    qkv_cols = partial_value.shape[1]
    packed = jnp.concatenate(
        [partial_value, squares[:, None], jnp.zeros((row_count, 127), jnp.float32)], axis=1
    )
    reduced = reduce_rows(packed)
    rows_per = row_count // page_devices
    my_rows = page_index * rows_per + jnp.arange(rows_per, dtype=jnp.int32)
    mine = finish_rows(
        reduced[:, :qkv_cols], reduced[:, qkv_cols], my_rows, prompt_len, num_seqs, local_heads
    )
    projected = gather_rows(mine.reshape(rows_per, qkv_cols)).reshape(
        row_count, local_heads, PER_KV + 2, HEAD_DIM
    )
    queries = projected[:, :, :PER_KV]
    fresh_kv = jnp.stack([projected[:, :, PER_KV], projected[:, :, PER_KV + 1]]).reshape(
        2, num_steps, num_seqs, kv_width
    )
    buffer = jnp.concatenate(
        [history, jnp.zeros((2, num_seqs, num_steps, kv_width), jnp.bfloat16)], axis=2
    )
    snapshots = []
    for step_index in range(num_steps):
        choose = parents[step_index][:, None] == jnp.arange(num_seqs, dtype=jnp.int32)[None, :]
        buffer = jnp.einsum(
            "nb,kbld->knld",
            choose.astype(jnp.bfloat16),
            buffer,
            preferred_element_type=jnp.float32,
        ).astype(jnp.bfloat16)
        buffer = lax.dynamic_update_slice(
            buffer, fresh_kv[:, step_index][:, :, None, :], (0, 0, PRIOR + step_index, 0)
        )
        snapshots.append(buffer)
    stacked = jnp.stack(snapshots)
    tail_keys = stacked[:, 0].reshape(num_steps, num_seqs, HISTORY, local_heads, HEAD_DIM)
    tail_vals = stacked[:, 1].reshape(num_steps, num_seqs, HISTORY, local_heads, HEAD_DIM)
    step_query = queries.reshape(num_steps, num_seqs, local_heads, PER_KV, HEAD_DIM)
    tail_len = PRIOR + 1 + jnp.arange(num_steps, dtype=jnp.int32)
    tail_valid = (jnp.arange(HISTORY, dtype=jnp.int32)[None, :] < tail_len[:, None])[
        :, None, None, None, :
    ]
    tail_scores = (
        jnp.einsum("tbkhd,tblkd->tbkhl", step_query, tail_keys, preferred_element_type=jnp.float32)
        * inv_root
    )
    tail_scores = jnp.where(tail_valid, tail_scores, NEGATIVE)
    tail_peak = jnp.max(tail_scores, axis=-1)
    tail_exp = jnp.where(tail_valid, jnp.exp(tail_scores - tail_peak[..., None]), 0.0)
    tail_total = jnp.sum(tail_exp, axis=-1)
    tail_acc = jnp.einsum(
        "tbkhl,tblkd->tbkhd",
        tail_exp.astype(jnp.bfloat16),
        tail_vals,
        preferred_element_type=jnp.float32,
    )
    tail_part = (tail_peak.reshape(-1), tail_total.reshape(-1), tail_acc.reshape(-1, HEAD_DIM))
    slot_rows = kv_pool.shape[1]
    slot_ids = page_index * slot_rows + jnp.arange(slot_rows, dtype=jnp.int32)
    matches = page_table[:, :, None] == slot_ids[None, None, :]
    slot_used = jnp.any(matches, axis=(0, 1))
    owner_group = jnp.sum(
        jnp.where(matches, jnp.arange(GROUPS, dtype=jnp.int32)[:, None, None], 0), axis=(0, 1)
    )
    page_number = jnp.sum(
        jnp.where(matches, jnp.arange(MAX_PAGES, dtype=jnp.int32)[None, :, None], 0), axis=(0, 1)
    )
    length = jnp.take(prompt_len, owner_group)
    live_tok = slot_used[:, None] & (
        page_number[:, None] * PAGE + jnp.arange(PAGE, dtype=jnp.int32)[None, :] < length[:, None]
    )
    live_full = live_tok[None, :, None, :]
    grouped = queries.reshape(num_steps, GROUPS, BEAMS, local_heads, PER_KV, HEAD_DIM)
    chosen = jnp.take(grouped, owner_group, axis=1)
    query_rows = num_steps * BEAMS * PER_KV
    chosen = jnp.transpose(chosen, (3, 1, 0, 2, 4, 5)).reshape(
        local_heads, slot_rows, query_rows, HEAD_DIM
    )
    page_keys = jnp.transpose(
        kv_pool[0].reshape(slot_rows, PAGE, local_heads, HEAD_DIM), (2, 0, 1, 3)
    )
    page_vals = jnp.transpose(
        kv_pool[1].reshape(slot_rows, PAGE, local_heads, HEAD_DIM), (2, 0, 1, 3)
    )
    scores = (
        jnp.einsum("ksqd,kspd->ksqp", chosen, page_keys, preferred_element_type=jnp.float32)
        * inv_root
    )
    scores = jnp.where(live_full, scores, NEGATIVE)
    slot_peak = jnp.max(scores, axis=-1)
    slot_exp = jnp.where(live_full, jnp.exp(scores - slot_peak[..., None]), 0.0)
    slot_total = jnp.sum(slot_exp, axis=-1)
    slot_acc = jnp.einsum(
        "ksqp,kspd->ksqd",
        slot_exp.astype(jnp.bfloat16),
        page_vals,
        preferred_element_type=jnp.float32,
    )
    member = (owner_group[:, None] == jnp.arange(GROUPS, dtype=jnp.int32)[None, :]) & slot_used[
        :, None
    ]
    spread = jnp.where(member[None, :, :, None], slot_peak[:, :, None, :], NEGATIVE)
    group_peak = jnp.max(spread, axis=1)
    slot_base = jnp.take(group_peak, owner_group, axis=1)
    weight = jnp.where(slot_used[None, :, None], jnp.exp(slot_peak - slot_base), 0.0)
    member_f = member.astype(jnp.float32)
    group_total = jnp.einsum(
        "sg,ksq->kgq", member_f, slot_total * weight, precision=lax.Precision.HIGHEST
    )
    group_acc = jnp.einsum(
        "sg,ksqd->kgqd", member_f, slot_acc * weight[..., None], precision=lax.Precision.HIGHEST
    )
    order_small = (2, 1, 3, 0, 4)
    peak_rows = jnp.transpose(
        group_peak.reshape(local_heads, GROUPS, num_steps, BEAMS, PER_KV), order_small
    )
    total_rows = jnp.transpose(
        group_total.reshape(local_heads, GROUPS, num_steps, BEAMS, PER_KV), order_small
    )
    acc_rows = jnp.transpose(
        group_acc.reshape(local_heads, GROUPS, num_steps, BEAMS, PER_KV, HEAD_DIM),
        (2, 1, 3, 0, 4, 5),
    )
    local_part = (peak_rows.reshape(-1), total_rows.reshape(-1), acc_rows.reshape(-1, HEAD_DIM))
    with_tail = combine(local_part, tail_part)
    first = page_index == 0
    part = jax.tree.map(lambda a, b: jnp.where(first, a, b), with_tail, local_part)
    attn_rows = part[0].shape[0]
    share = attn_rows // page_devices
    sent = pack_blocks(
        part[0].reshape(outer_count, inner_count, share),
        part[1].reshape(outer_count, inner_count, share),
        part[2].reshape(outer_count, inner_count, share, HEAD_DIM),
        share,
    )
    stage = merge_blocks(lax.all_to_all(sent, "px", 0, 0, tiled=False), share)
    sent = pack_blocks(*stage, share)
    top, total, acc = merge_blocks(lax.all_to_all(sent, "pz", 0, 0, tiled=False), share)
    attended_mine = (acc / total[:, None]).astype(jnp.bfloat16)
    attended = gather_rows(attended_mine)
    flat_heads = attended.reshape(row_count, local_heads * PER_KV * HEAD_DIM)
    head_terms = jnp.dot(flat_heads, w_out, preferred_element_type=jnp.float32)
    shared = gather_all(head_terms.astype(jnp.bfloat16), "kv").astype(jnp.float32)
    mixed_out = jnp.sum(shared, axis=0) + widened
    return (mixed_out.astype(jnp.bfloat16).reshape(num_steps, num_seqs, -1), buffer)


def solution(mesh):
    row = mesh.devices[0]
    outer = len({device.coords[0] for device in row})
    split = Mesh(
        mesh.devices.reshape(mesh.devices.shape[0], outer, row.size // outer), ("kv", "px", "pz")
    )
    pages = ("px", "pz")
    placed = (
        P(),
        P(),
        P(),
        P(),
        P("kv", pages),
        P(pages),
        P(pages, "kv"),
        P("kv", pages),
        P(None, None, None, "kv"),
        P(None, pages, None, "kv"),
    )
    return jax.shard_map(
        per_device,
        mesh=split,
        in_specs=placed,
        out_specs=(P(None, None, pages), P(None, None, None, "kv")),
        check_vma=False,
    )
```
